256 devices in a mesh: ctx: 32 (over y, z), head: 8 (over x, core).
Axes of the slice: x: 4, y: 4, z: 8, core: 2. Of those that a mesh axis runs over, the one named last changes fastest.
Arguments:
- queries: bfloat16 [4096, 4096], P('ctx', 'head'), may hold values from -30 to 30
- key_proj: bfloat16 [4096, 1024], P('ctx', 'head'), may hold values from -6 to 6
- value_proj: bfloat16 [4096, 1024], P('ctx', 'head'), may hold values from -6 to 6
- lengths: int32 [32], replicated, may hold values from 1 to 2048, 4096 in all
- out_weight: bfloat16 [4096, 8192], P(None, 'head'), may hold values from -0.09375 to 0.09375
Outputs:
- mixed_out: bfloat16 [4096, 8192], P('ctx', 'head')
The draws below stay inside these ranges and needn't reach their ends.
Inputs may be any that keep to these rules, and one draw needn't show every extreme that they name: Document lengths in pack order; they sum to 4096 and the longest is exactly 2048.
All inputs are finite; a program needn't handle non-finite values.
Results may differ from the reference program's by a relative error of at most 0.005.
The reference program's roundings to bfloat16 on the way (of `q_rot`, `k_rot`, `expo` and `attended`) count: a program that leaves them out, or rounds other values in their place, can miss the bound.
Values may be sent and summed in bfloat16 or wider, within the bound.
No kernel may reach another device: no remote copies, remote signals or barrier semaphores. Data moves between devices by JAX's collectives and lax.ppermute only.
A program may use at most 64 MiB of HBM per device.

```python
import math
import jax
import jax.numpy as jnp
import numpy as np
from jax import lax

D = 8192
HQ = 32
KVH = 8
HD = 128
TOK_DEV = 128
TOKENS = 4096
MOST = 2048
DOCS = 32


def paired_draw(key):
    base_key = jax.random.fold_in(key, 29)
    key_query, key_key = jax.random.split(base_key, 2)
    queries = jnp.clip(jax.random.normal(key_query, (TOKENS, HQ * HD), jnp.float32), -6.0, 6.0)
    key_rows = jnp.clip(jax.random.normal(key_key, (TOKENS, KVH * HD), jnp.float32), -6.0, 6.0)
    return (queries, key_rows)


def draw_queries(key, part):
    return paired_draw(key)[0].astype(jnp.bfloat16)


def draw_key_proj(key, part):
    return paired_draw(key)[1].astype(jnp.bfloat16)


def block_levels(rng, dims, cuts, smallest, largest):
    gain, own = 1.0, jax.random.fold_in(rng, 6)
    for dim, blocks in cuts:
        steps = jnp.exp(jax.random.uniform(jax.random.fold_in(own, dim), (blocks,), jnp.float32, smallest / len(cuts), largest / len(cuts)))
        gain = gain * jnp.repeat(steps, dims[dim] // blocks).reshape([-1 if axis == dim else 1 for axis in range(len(dims))])
    return gain


def length_profile(count, total, bound, lean):
    weights = [(1 << 20) // math.isqrt(standing ** lean) + 1 for standing in range(2, count + 1)]
    rest, given = total - bound - (count - 1), [1] * (count - 1)
    while rest > 0:
        movable = [i for i in range(count - 1) if given[i] < bound]
        mass, remaining = sum([weights[i] for i in movable]), rest
        for i in movable:
            extra = min(bound - given[i], max(1, remaining * weights[i] // mass), rest)
            given[i] = given[i] + extra
            rest = rest - extra
    return np.array([bound] + given)


def ragged(own_key, number_of, total, limit, lean):
    if number_of == 2:
        one = jax.random.randint(own_key, (), max(1, total - limit), min(limit, total - 1) + 1)
        return jnp.stack([one, total - one])
    sizes = jnp.asarray(length_profile(number_of, total, limit, lean), jnp.int32)
    couples = (number_of - 1) // 2
    giver, taker = sizes[1:1 + 2 * couples:2], sizes[2:2 + 2 * couples:2]
    margin = jnp.minimum(giver - 1, limit - taker)
    moved = jax.random.randint(jax.random.fold_in(own_key, 1), (couples,), 0, 1 << 20) % (margin + 1)
    sizes = sizes.at[1:1 + 2 * couples:2].set(giver - moved).at[2:2 + 2 * couples:2].set(taker + moved)
    return sizes[jax.random.permutation(jax.random.fold_in(own_key, 2), number_of)]


def noise(stream_key, dims, deviation, limit, cuts=(), kind=jnp.bfloat16):
    result = jax.random.normal(stream_key, dims, jnp.float32) * deviation
    if len(cuts) > 0:
        result = block_levels(stream_key, dims, cuts, -0.22, 0.18) * result
    return jnp.clip(result, min=-limit, max=limit).astype(kind)


def setup_inputs(seed: int = 0) -> dict:
    key_of = jax.random.split(jax.random.key(seed), 6)
    return {
        "queries": draw_queries(jax.random.fold_in(key_of[5], 71), 0),
        "key_proj": draw_key_proj(jax.random.fold_in(key_of[5], 71), 0),
        "value_proj": noise(key_of[2], (TOKENS, KVH * HD), 1.0, 6.0, ((0, 32), (1, 8))),
        "lengths": ragged(key_of[3], DOCS, TOKENS, MOST, 2).astype(jnp.int32),
        "out_weight": noise(key_of[4], (HQ * HD, D), (HQ * HD) ** -0.5, 0.09375, ((1, 8),)),
    }


rope_theta = 500000.0

def doc_starts(lengths, positions):
    doc_ends = jnp.cumsum(lengths)
    picked = jnp.where(doc_ends[None, :] <= positions[:, None], lengths[None, :], 0)
    return lax.optimization_barrier(jnp.sum(picked, axis=1)).astype(jnp.int32)

def rotary(projected, offsets, head_dim):
    token_count = projected.shape[0]
    heads_grid = projected.astype(jnp.float32).reshape(token_count, -1, head_dim)
    half_dim = head_dim // 2
    inverse = rope_theta ** (-2.0 * jnp.arange(half_dim).astype(jnp.float32) / head_dim)
    angles = offsets.astype(jnp.float32)[:, None] * inverse[None, :]
    cosine = jnp.cos(angles)[:, None, :]
    sine_part = jnp.sin(angles)[:, None, :]
    first_half = heads_grid[..., :half_dim]
    second_half = heads_grid[..., half_dim:]
    rotated = jnp.concatenate([first_half * cosine - second_half * sine_part, second_half * cosine + first_half * sine_part], axis=-1)
    return rotated.reshape(token_count, -1).astype(jnp.bfloat16)

def reference(queries, key_proj, value_proj, lengths, out_weight):
    positions = jnp.arange(TOKENS, dtype=jnp.int32)
    starts = doc_starts(lengths, positions)
    offsets = positions - starts
    q_rot = rotary(queries, offsets, HD)
    k_rot = rotary(key_proj, offsets, HD)
    query_group = HQ // KVH
    window = min(MOST + TOK_DEV, TOKENS)
    blocks = TOKENS // TOK_DEV

    def one_block(block_index):
        q_begin = (block_index * TOK_DEV).astype(jnp.int32)
        k_begin = jnp.clip(q_begin - MOST, 0, TOKENS - window).astype(jnp.int32)
        q_block = lax.dynamic_slice_in_dim(q_rot, q_begin, TOK_DEV, 0).reshape(TOK_DEV, KVH, query_group, HD)
        k_block = lax.dynamic_slice_in_dim(k_rot, k_begin, window, 0).reshape(window, KVH, HD)
        v_block = lax.dynamic_slice_in_dim(value_proj, k_begin, window, 0).reshape(window, KVH, HD)
        q_pos = q_begin + jnp.arange(TOK_DEV, dtype=jnp.int32)
        k_pos = k_begin + jnp.arange(window, dtype=jnp.int32)
        q_doc = lax.dynamic_slice_in_dim(starts, q_begin, TOK_DEV, 0)
        allowed = (k_pos[None, :] <= q_pos[:, None]) & (k_pos[None, :] >= q_doc[:, None])

        def one_head(head_index):
            q_head = jnp.take(q_block, head_index, axis=1).astype(jnp.float32)
            k_head = jnp.take(k_block, head_index, axis=1).astype(jnp.float32)
            v_head = jnp.take(v_block, head_index, axis=1).astype(jnp.float32)
            scores = jnp.einsum('tgd,nd->gtn', q_head, k_head) / jnp.sqrt(jnp.float32(HD))
            scores = jnp.where(allowed[None], scores, -jnp.inf)
            row_max = lax.optimization_barrier(jnp.max(scores, axis=-1, keepdims=True))
            expo = jnp.exp(scores - row_max)
            row_sum = lax.optimization_barrier(jnp.sum(expo, axis=-1, keepdims=True))
            rounded = lax.optimization_barrier(expo.astype(jnp.bfloat16)).astype(jnp.float32)
            weighted = jnp.einsum('gtn,nd->gtd', rounded, v_head) / row_sum
            return jnp.transpose(weighted, (1, 0, 2))
        per_head = lax.map(one_head, jnp.arange(KVH, dtype=jnp.int32))
        return jnp.transpose(per_head, (1, 0, 2, 3)).reshape(TOK_DEV, HQ * HD).astype(jnp.bfloat16)
    attended = lax.map(one_block, jnp.arange(blocks, dtype=jnp.int32)).reshape(TOKENS, HQ * HD)
    return jnp.dot(attended, out_weight, preferred_element_type=jnp.float32).astype(jnp.bfloat16)
```

```python
import jax
import jax.numpy as jnp
from jax import lax
from jax.sharding import PartitionSpec as P

HD = 128
MOST = 2048


rope_theta = 500000.0


def doc_starts(lengths, positions):
    doc_ends = jnp.cumsum(lengths)
    picked = jnp.where(doc_ends[None, :] <= positions[:, None], lengths[None, :], 0)
    return jnp.sum(picked, axis=1)


def rotary(projected, offsets, head_dim):
    token_count = projected.shape[0]
    heads_grid = projected.astype(jnp.float32).reshape(token_count, -1, head_dim)
    half_dim = head_dim // 2
    inverse = rope_theta ** (-2.0 * jnp.arange(half_dim).astype(jnp.float32) / head_dim)
    angles = offsets.astype(jnp.float32)[:, None] * inverse[None, :]
    cosine = jnp.cos(angles)[:, None, :]
    sine_part = jnp.sin(angles)[:, None, :]
    first_half = heads_grid[..., :half_dim]
    second_half = heads_grid[..., half_dim:]
    rotated = jnp.concatenate(
        [
            first_half * cosine - second_half * sine_part,
            second_half * cosine + first_half * sine_part,
        ],
        axis=-1,
    )
    return rotated.reshape(token_count, -1).astype(jnp.bfloat16)


def make_body(n_ctx, n_head, row):
    def on_device(queries, key_proj, value_proj, lengths, out_weight):
        tok_rows = queries.shape[0]
        kv_width = key_proj.shape[1]
        kv_local = kv_width // HD
        query_group = queries.shape[1] // kv_width
        back = -(-(MOST - 1) // tok_rows)
        rows_back = -(-back // row)
        span = rows_back * row
        ctx = lax.axis_index("ctx")
        first_row = ctx * tok_rows
        positions = first_row + jnp.arange(tok_rows, dtype=jnp.int32)
        starts = doc_starts(lengths, positions)
        offsets = positions - starts
        q_rot = rotary(queries, offsets, HD).reshape(tok_rows, kv_local, query_group, HD)
        k_rot = rotary(key_proj, offsets, HD)
        own = jnp.concatenate([k_rot, value_proj], axis=1)

        bundle = [own]
        for m in range(1, rows_back + 1):
            shift = row * m
            bundle.append(lax.ppermute(own, "ctx", [(s, s + shift) for s in range(n_ctx - shift)]))
        bundle = jnp.stack(bundle)
        blocks = {row * m: bundle[m] for m in range(rows_back + 1)}
        z = ctx % row
        for b in range(1, row):
            lo = jnp.where(z + b >= row, 1, 0)
            piece = lax.dynamic_slice_in_dim(bundle, lo, rows_back, 0)
            pairs = [(r * row + s, r * row + (s + b) % row) for r in range(n_ctx // row) for s in range(row)]
            got = lax.ppermute(piece, "ctx", pairs)
            for m in range(rows_back):
                blocks[b + row * m] = got[m]
        window = jnp.concatenate([blocks[span - k] for k in range(span + 1)], axis=0)
        key_count = window.shape[0]
        key_block = window[:, :kv_width].reshape(key_count, kv_local, HD)
        value_block = window[:, kv_width:].reshape(key_count, kv_local, HD)

        scores = jnp.einsum(
            "tkgd,nkd->kgtn", q_rot, key_block, preferred_element_type=jnp.float32
        ) / jnp.sqrt(jnp.float32(HD))
        key_pos = (ctx - span) * tok_rows + jnp.arange(key_count, dtype=jnp.int32)
        allowed = (key_pos[None, :] <= positions[:, None]) & (key_pos[None, :] >= starts[:, None])
        scores = jnp.where(allowed, scores, -1e30)
        row_max = jnp.max(scores, axis=-1)
        weights = jnp.where(allowed, jnp.exp(scores - row_max[..., None]), 0.0)
        row_sum = jnp.sum(weights, axis=-1)
        weighted = jnp.einsum(
            "kgtn,nkd->kgtd",
            weights.astype(jnp.bfloat16),
            value_block,
            preferred_element_type=jnp.float32,
        )
        normed = (weighted / row_sum[..., None]).astype(jnp.bfloat16)
        attended = jnp.transpose(normed, (2, 0, 1, 3)).reshape(tok_rows, kv_local * query_group * HD)

        feat = attended.shape[1]
        head = lax.axis_index("head")
        total = jnp.dot(
            attended,
            lax.dynamic_slice_in_dim(out_weight, head * feat, feat, 0),
            preferred_element_type=jnp.float32,
        )
        for d in range(1, n_head):
            got = lax.ppermute(attended, "head", [(s, (s + d) % n_head) for s in range(n_head)])
            src = (head - d) % n_head
            total = total + jnp.dot(
                got,
                lax.dynamic_slice_in_dim(out_weight, src * feat, feat, 0),
                preferred_element_type=jnp.float32,
            )
        return total.astype(jnp.bfloat16)

    return on_device


def solution(mesh):
    n_ctx, n_head = mesh.shape["ctx"], mesh.shape["head"]
    row = 8 if n_ctx % 8 == 0 else n_ctx
    placed = (P("ctx", "head"), P("ctx", "head"), P("ctx", "head"), P(), P(None, "head"))
    return jax.shard_map(
        make_body(n_ctx, n_head, row), mesh=mesh, in_specs=placed, out_specs=P("ctx", "head"), check_vma=False
    )
```

```python
import jax
import jax.numpy as jnp
from jax import lax
from jax.sharding import PartitionSpec as P

HD = 128
MOST = 2048


rope_theta = 500000.0


def doc_starts(lengths, positions):
    doc_ends = jnp.cumsum(lengths)
    picked = jnp.where(doc_ends[None, :] <= positions[:, None], lengths[None, :], 0)
    return jnp.sum(picked, axis=1)


def rotary(projected, offsets, head_dim):
    token_count = projected.shape[0]
    heads_grid = projected.astype(jnp.float32).reshape(token_count, -1, head_dim)
    half_dim = head_dim // 2
    inverse = rope_theta ** (-2.0 * jnp.arange(half_dim).astype(jnp.float32) / head_dim)
    angles = offsets.astype(jnp.float32)[:, None] * inverse[None, :]
    cosine = jnp.cos(angles)[:, None, :]
    sine_part = jnp.sin(angles)[:, None, :]
    first_half = heads_grid[..., :half_dim]
    second_half = heads_grid[..., half_dim:]
    rotated = jnp.concatenate(
        [
            first_half * cosine - second_half * sine_part,
            second_half * cosine + first_half * sine_part,
        ],
        axis=-1,
    )
    return rotated.reshape(token_count, -1).astype(jnp.bfloat16)


def make_body(n_ctx, n_head, row):
    def on_device(queries, key_proj, value_proj, lengths, out_weight):
        tok_rows = queries.shape[0]
        kv_width = key_proj.shape[1]
        kv_local = kv_width // HD
        query_group = queries.shape[1] // kv_width
        back = -(-(MOST - 1) // tok_rows)
        rows_back = -(-back // row)
        span = rows_back * row
        ctx = lax.axis_index("ctx")
        first_row = ctx * tok_rows
        positions = first_row + jnp.arange(tok_rows, dtype=jnp.int32)
        starts = doc_starts(lengths, positions)
        offsets = positions - starts
        q_rot = rotary(queries, offsets, HD).reshape(tok_rows, kv_local, query_group, HD)
        k_rot = rotary(key_proj, offsets, HD)
        own = jnp.concatenate([k_rot, value_proj], axis=1)

        bundle = [own]
        for m in range(1, rows_back + 1):
            shift = row * m
            bundle.append(lax.ppermute(own, "ctx", [(s, s + shift) for s in range(n_ctx - shift)]))
        blocks = {row * m: bundle[m] for m in range(rows_back + 1)}
        bundle = jnp.stack(bundle)
        z = ctx % row
        n_rows = n_ctx // row
        ahead = [(r * row + s, r * row + (s + 1) % row) for r in range(n_rows) for s in range(row)]
        behind = [(r * row + s, r * row + (s - 1) % row) for r in range(n_rows) for s in range(row)]

        def take(packet, b):
            lo = jnp.where(z < b, 1, 0)
            got = lax.dynamic_slice_in_dim(packet, lo, rows_back, 0)
            for m in range(rows_back):
                blocks[b + row * m] = got[m]

        forward, backward = bundle, bundle
        for step in range(1, row // 2 + 1):
            forward = lax.ppermute(forward, "ctx", ahead)
            take(forward, step)
            if step < row - row // 2:
                backward = lax.ppermute(backward, "ctx", behind)
                take(backward, row - step)
        window = jnp.concatenate([blocks[span - k] for k in range(span + 1)], axis=0)
        key_count = window.shape[0]
        key_block = window[:, :kv_width].reshape(key_count, kv_local, HD)
        value_block = window[:, kv_width:].reshape(key_count, kv_local, HD)

        scores = jnp.einsum(
            "tkgd,nkd->kgtn", q_rot, key_block, preferred_element_type=jnp.float32
        ) / jnp.sqrt(jnp.float32(HD))
        key_pos = (ctx - span) * tok_rows + jnp.arange(key_count, dtype=jnp.int32)
        allowed = (key_pos[None, :] <= positions[:, None]) & (key_pos[None, :] >= starts[:, None])
        scores = jnp.where(allowed, scores, -1e30)
        row_max = jnp.max(scores, axis=-1)
        weights = jnp.where(allowed, jnp.exp(scores - row_max[..., None]), 0.0)
        row_sum = jnp.sum(weights, axis=-1)
        weighted = jnp.einsum(
            "kgtn,nkd->kgtd",
            weights.astype(jnp.bfloat16),
            value_block,
            preferred_element_type=jnp.float32,
        )
        normed = (weighted / row_sum[..., None]).astype(jnp.bfloat16)
        attended = jnp.transpose(normed, (2, 0, 1, 3)).reshape(tok_rows, kv_local * query_group * HD)

        feat = attended.shape[1]
        head = lax.axis_index("head")
        core = head % 2

        def project(piece, src):
            rows = lax.dynamic_slice_in_dim(out_weight, src * feat, feat, 0)
            return jnp.dot(piece, rows, preferred_element_type=jnp.float32)

        up = lax.ppermute(attended, "head", [(s, (s + 2) % n_head) for s in range(n_head)])
        down = lax.ppermute(attended, "head", [(s, (s - 2) % n_head) for s in range(n_head)])
        swap = [(s, s ^ 1) for s in range(n_head)]
        partner = lax.ppermute(attended, "head", swap)
        relay_pairs = [(s, (s + 2) % n_head) if s % 2 == 0 else (s, (s - 2) % n_head) for s in range(n_head)]
        far = lax.ppermute(jnp.where(core == 0, up, down), "head", relay_pairs)
        near_other = lax.ppermute(jnp.stack([up, down]), "head", swap)
        far_other = lax.ppermute(far, "head", swap)
        other = head ^ 1
        total = project(attended, head)
        total = total + project(up, (head - 2) % n_head)
        total = total + project(down, (head + 2) % n_head)
        total = total + project(partner, other)
        total = total + project(far, (head + 4) % n_head)
        total = total + project(near_other[0], (other - 2) % n_head)
        total = total + project(near_other[1], (other + 2) % n_head)
        total = total + project(far_other, (other + 4) % n_head)
        return total.astype(jnp.bfloat16)

    return on_device


def solution(mesh):
    n_ctx, n_head = mesh.shape["ctx"], mesh.shape["head"]
    row = 8 if n_ctx % 8 == 0 else n_ctx
    placed = (P("ctx", "head"), P("ctx", "head"), P("ctx", "head"), P(), P(None, "head"))
    return jax.shard_map(
        make_body(n_ctx, n_head, row), mesh=mesh, in_specs=placed, out_specs=P("ctx", "head"), check_vma=False
    )
```

```python
import jax
import jax.numpy as jnp
from jax import lax
from jax.sharding import PartitionSpec as P

HD = 128
MOST = 2048


rope_theta = 500000.0


def doc_starts(lengths, positions):
    doc_ends = jnp.cumsum(lengths)
    picked = jnp.where(doc_ends[None, :] <= positions[:, None], lengths[None, :], 0)
    return jnp.sum(picked, axis=1)


def rotary(projected, offsets, head_dim):
    token_count = projected.shape[0]
    heads_grid = projected.astype(jnp.float32).reshape(token_count, -1, head_dim)
    half_dim = head_dim // 2
    inverse = rope_theta ** (-2.0 * jnp.arange(half_dim).astype(jnp.float32) / head_dim)
    angles = offsets.astype(jnp.float32)[:, None] * inverse[None, :]
    cosine = jnp.cos(angles)[:, None, :]
    sine_part = jnp.sin(angles)[:, None, :]
    first_half = heads_grid[..., :half_dim]
    second_half = heads_grid[..., half_dim:]
    rotated = jnp.concatenate(
        [
            first_half * cosine - second_half * sine_part,
            second_half * cosine + first_half * sine_part,
        ],
        axis=-1,
    )
    return rotated.reshape(token_count, -1).astype(jnp.bfloat16)


def make_body(n_ctx, n_head, row):
    def on_device(queries, key_proj, value_proj, lengths, out_weight):
        tok_rows = queries.shape[0]
        kv_width = key_proj.shape[1]
        kv_local = kv_width // HD
        query_group = queries.shape[1] // kv_width
        back = -(-(MOST - 1) // tok_rows)
        rows_back = -(-back // row)
        span = rows_back * row
        ctx = lax.axis_index("ctx")
        first_row = ctx * tok_rows
        positions = first_row + jnp.arange(tok_rows, dtype=jnp.int32)
        starts = doc_starts(lengths, positions)
        offsets = positions - starts
        q_rot = rotary(queries, offsets, HD).reshape(tok_rows, kv_local, query_group, HD)
        own = jnp.concatenate([key_proj, value_proj], axis=1)

        def rotate_keys(block, k):
            pos = (ctx - k) * tok_rows + jnp.arange(tok_rows, dtype=jnp.int32)
            k_rot = rotary(block[:, :kv_width], pos - doc_starts(lengths, pos), HD)
            return jnp.concatenate([k_rot, block[:, kv_width:]], axis=1)

        bundle = [own]
        for m in range(1, rows_back + 1):
            shift = row * m
            bundle.append(lax.ppermute(own, "ctx", [(s, s + shift) for s in range(n_ctx - shift)]))
        blocks = {row * m: bundle[m] for m in range(rows_back + 1)}
        bundle = jnp.stack(bundle)
        z = ctx % row
        n_rows = n_ctx // row
        ahead = [(r * row + s, r * row + (s + 1) % row) for r in range(n_rows) for s in range(row)]
        behind = [(r * row + s, r * row + (s - 1) % row) for r in range(n_rows) for s in range(row)]

        def take(packet, b):
            lo = jnp.where(z < b, 1, 0)
            got = lax.dynamic_slice_in_dim(packet, lo, rows_back, 0)
            for m in range(rows_back):
                blocks[b + row * m] = got[m]

        forward, backward = bundle, bundle
        for step in range(1, row // 2 + 1):
            forward = lax.ppermute(forward, "ctx", ahead)
            take(forward, step)
            if step < row - row // 2:
                backward = lax.ppermute(backward, "ctx", behind)
                take(backward, row - step)
        window = jnp.concatenate([rotate_keys(blocks[span - k], span - k) for k in range(span + 1)], axis=0)
        key_count = window.shape[0]
        key_block = window[:, :kv_width].reshape(key_count, kv_local, HD)
        value_block = window[:, kv_width:].reshape(key_count, kv_local, HD)

        scores = jnp.einsum(
            "tkgd,nkd->kgtn", q_rot, key_block, preferred_element_type=jnp.float32
        ) / jnp.sqrt(jnp.float32(HD))
        key_pos = (ctx - span) * tok_rows + jnp.arange(key_count, dtype=jnp.int32)
        allowed = (key_pos[None, :] <= positions[:, None]) & (key_pos[None, :] >= starts[:, None])
        scores = jnp.where(allowed, scores, -1e30)
        row_max = jnp.max(scores, axis=-1)
        weights = jnp.where(allowed, jnp.exp(scores - row_max[..., None]), 0.0)
        row_sum = jnp.sum(weights, axis=-1)
        weighted = jnp.einsum(
            "kgtn,nkd->kgtd",
            weights.astype(jnp.bfloat16),
            value_block,
            preferred_element_type=jnp.float32,
        )
        normed = (weighted / row_sum[..., None]).astype(jnp.bfloat16)
        attended = jnp.transpose(normed, (2, 0, 1, 3)).reshape(tok_rows, kv_local * query_group * HD)

        feat = attended.shape[1]
        head = lax.axis_index("head")
        core = head % 2

        def project(piece, src):
            rows = lax.dynamic_slice_in_dim(out_weight, src * feat, feat, 0)
            return jnp.dot(piece, rows, preferred_element_type=jnp.float32)

        up = lax.ppermute(attended, "head", [(s, (s + 2) % n_head) for s in range(n_head)])
        down = lax.ppermute(attended, "head", [(s, (s - 2) % n_head) for s in range(n_head)])
        swap = [(s, s ^ 1) for s in range(n_head)]
        partner = lax.ppermute(attended, "head", swap)
        relay_pairs = [(s, (s + 2) % n_head) if s % 2 == 0 else (s, (s - 2) % n_head) for s in range(n_head)]
        far = lax.ppermute(jnp.where(core == 0, up, down), "head", relay_pairs)
        near_other = lax.ppermute(jnp.stack([up, down]), "head", swap)
        far_other = lax.ppermute(far, "head", swap)
        other = head ^ 1
        total = project(attended, head)
        total = total + project(up, (head - 2) % n_head)
        total = total + project(down, (head + 2) % n_head)
        total = total + project(partner, other)
        total = total + project(far, (head + 4) % n_head)
        total = total + project(near_other[0], (other - 2) % n_head)
        total = total + project(near_other[1], (other + 2) % n_head)
        total = total + project(far_other, (other + 4) % n_head)
        return total.astype(jnp.bfloat16)

    return on_device


def solution(mesh):
    n_ctx, n_head = mesh.shape["ctx"], mesh.shape["head"]
    row = 8 if n_ctx % 8 == 0 else n_ctx
    placed = (P("ctx", "head"), P("ctx", "head"), P("ctx", "head"), P(), P(None, "head"))
    return jax.shard_map(
        make_body(n_ctx, n_head, row), mesh=mesh, in_specs=placed, out_specs=P("ctx", "head"), check_vma=False
    )
```

```python
import jax
import jax.numpy as jnp
from jax import lax
from jax.sharding import PartitionSpec as P

HD = 128
MOST = 2048


rope_theta = 500000.0


def doc_starts(lengths, positions):
    doc_ends = jnp.cumsum(lengths)
    picked = jnp.where(doc_ends[None, :] <= positions[:, None], lengths[None, :], 0)
    return jnp.sum(picked, axis=1)


def rotary(projected, offsets, head_dim):
    token_count = projected.shape[0]
    heads_grid = projected.astype(jnp.float32).reshape(token_count, -1, head_dim)
    half_dim = head_dim // 2
    inverse = rope_theta ** (-2.0 * jnp.arange(half_dim).astype(jnp.float32) / head_dim)
    angles = offsets.astype(jnp.float32)[:, None] * inverse[None, :]
    cosine = jnp.cos(angles)[:, None, :]
    sine_part = jnp.sin(angles)[:, None, :]
    first_half = heads_grid[..., :half_dim]
    second_half = heads_grid[..., half_dim:]
    rotated = jnp.concatenate(
        [
            first_half * cosine - second_half * sine_part,
            second_half * cosine + first_half * sine_part,
        ],
        axis=-1,
    )
    return rotated.reshape(token_count, -1).astype(jnp.bfloat16)


def make_body(n_ctx, n_head, row):
    def on_device(queries, key_proj, value_proj, lengths, out_weight):
        tok_rows = queries.shape[0]
        kv_width = key_proj.shape[1]
        kv_local = kv_width // HD
        query_group = queries.shape[1] // kv_width
        back = -(-(MOST - 1) // tok_rows)
        rows_back = -(-back // row)
        span = rows_back * row
        ctx = lax.axis_index("ctx")
        first_row = ctx * tok_rows
        positions = first_row + jnp.arange(tok_rows, dtype=jnp.int32)
        starts = doc_starts(lengths, positions)
        offsets = positions - starts
        q_rot = rotary(queries, offsets, HD).reshape(tok_rows, kv_local, query_group, HD)
        k_rot = rotary(key_proj, offsets, HD)
        own = jnp.concatenate([k_rot, value_proj], axis=1)

        bundle = [own]
        for m in range(1, rows_back + 1):
            shift = row * m
            bundle.append(lax.ppermute(own, "ctx", [(s, s + shift) for s in range(n_ctx - shift)]))
        blocks = {row * m: bundle[m] for m in range(rows_back + 1)}
        bundle = jnp.stack(bundle)
        z = ctx % row
        n_rows = n_ctx // row
        for chain in relay_plan(row, rows_back):
            packet = bundle
            for step in chain:
                lo = jnp.asarray(step["send"], jnp.int32)[z]
                packet = lax.ppermute(
                    lax.dynamic_slice_in_dim(packet, lo, step["width"], 0),
                    "ctx",
                    [(r * row + s, r * row + (s + step["dir"]) % row) for r in range(n_rows) for s in range(row)],
                )
                at = jnp.asarray(step["take"], jnp.int32)[z]
                got = lax.dynamic_slice_in_dim(packet, at, len(step["blocks"]), 0)
                for i, blk in enumerate(step["blocks"]):
                    blocks[blk] = got[i]
        window = jnp.concatenate([blocks[span - k] for k in range(span + 1)], axis=0)
        key_count = window.shape[0]
        key_block = window[:, :kv_width].reshape(key_count, kv_local, HD)
        value_block = window[:, kv_width:].reshape(key_count, kv_local, HD)

        scores = jnp.einsum(
            "tkgd,nkd->kgtn", q_rot, key_block, preferred_element_type=jnp.float32
        ) / jnp.sqrt(jnp.float32(HD))
        key_pos = (ctx - span) * tok_rows + jnp.arange(key_count, dtype=jnp.int32)
        allowed = (key_pos[None, :] <= positions[:, None]) & (key_pos[None, :] >= starts[:, None])
        scores = jnp.where(allowed, scores, -1e30)
        row_max = jnp.max(scores, axis=-1)
        weights = jnp.where(allowed, jnp.exp(scores - row_max[..., None]), 0.0)
        row_sum = jnp.sum(weights, axis=-1)
        weighted = jnp.einsum(
            "kgtn,nkd->kgtd",
            weights.astype(jnp.bfloat16),
            value_block,
            preferred_element_type=jnp.float32,
        )
        normed = (weighted / row_sum[..., None]).astype(jnp.bfloat16)
        attended = jnp.transpose(normed, (2, 0, 1, 3)).reshape(tok_rows, kv_local * query_group * HD)

        feat = attended.shape[1]
        head = lax.axis_index("head")
        core = head % 2

        def project(piece, src):
            rows = lax.dynamic_slice_in_dim(out_weight, src * feat, feat, 0)
            return jnp.dot(piece, rows, preferred_element_type=jnp.float32)

        up = lax.ppermute(attended, "head", [(s, (s + 2) % n_head) for s in range(n_head)])
        down = lax.ppermute(attended, "head", [(s, (s - 2) % n_head) for s in range(n_head)])
        swap = [(s, s ^ 1) for s in range(n_head)]
        partner = lax.ppermute(attended, "head", swap)
        relay_pairs = [(s, (s + 2) % n_head) if s % 2 == 0 else (s, (s - 2) % n_head) for s in range(n_head)]
        far = lax.ppermute(jnp.where(core == 0, up, down), "head", relay_pairs)
        near_other = lax.ppermute(jnp.stack([up, down]), "head", swap)
        far_other = lax.ppermute(far, "head", swap)
        other = head ^ 1
        total = project(attended, head)
        total = total + project(up, (head - 2) % n_head)
        total = total + project(down, (head + 2) % n_head)
        total = total + project(partner, other)
        total = total + project(far, (head + 4) % n_head)
        total = total + project(near_other[0], (other - 2) % n_head)
        total = total + project(near_other[1], (other + 2) % n_head)
        total = total + project(far_other, (other + 4) % n_head)
        return total.astype(jnp.bfloat16)

    return on_device


def relay_plan(row, rows_back):
    half = row // 2
    split = row % 2 == 0

    def part(z, b, direction):
        lo = 1 if z < b else 0
        slots = list(range(lo, lo + rows_back))
        if split and b == half:
            cut = (rows_back + 1) // 2
            slots = slots[:cut] if direction == 1 else slots[cut:]
        return slots

    chains = []
    for direction in (1, -1):
        rounds = range(1, half + 1) if direction == 1 else range(1, (half if split else row - 1 - half) + 1)
        bs = [r if direction == 1 else row - r for r in rounds]
        steps, held = [], None
        for i, b in enumerate(bs):
            need = {}
            for n in range(row):
                source = (n - direction * i) % row
                slots = set()
                for later in bs[i:]:
                    receiver = (source + later) % row
                    slots.update(part(receiver, later, direction))
                need[n] = slots
            width = max(max(v) - min(v) + 1 for v in need.values())
            lo = {n: min(min(v), rows_back + 1 - width) for n, v in need.items()}
            send = []
            for z in range(row):
                offset = lo[z] - (0 if held is None else held[(z - direction) % row])
                assert 0 <= offset and offset + width <= (rows_back + 1 if held is None else steps[-1]["width"])
                send.append(offset)
            take, blocks = [], None
            for z in range(row):
                sender = (z - direction) % row
                slots = part(z, b, direction)
                take.append(slots[0] - lo[sender])
                lo_z = 1 if z < b else 0
                mine = [b + row * (m - lo_z) for m in slots]
                assert blocks is None or blocks == mine
                blocks = mine
            steps.append({"dir": direction, "width": width, "send": send, "take": take, "blocks": blocks})
            held = lo
        chains.append(steps)
    return chains


def solution(mesh):
    n_ctx, n_head = mesh.shape["ctx"], mesh.shape["head"]
    row = 8 if n_ctx % 8 == 0 else n_ctx
    placed = (P("ctx", "head"), P("ctx", "head"), P("ctx", "head"), P(), P(None, "head"))
    return jax.shard_map(
        make_body(n_ctx, n_head, row), mesh=mesh, in_specs=placed, out_specs=P("ctx", "head"), check_vma=False
    )
```

```python
import jax
import jax.numpy as jnp
from jax import lax
from jax.sharding import PartitionSpec as P

HD = 128
MOST = 2048


rope_theta = 500000.0


def doc_starts(lengths, positions):
    doc_ends = jnp.cumsum(lengths)
    picked = jnp.where(doc_ends[None, :] <= positions[:, None], lengths[None, :], 0)
    return jnp.sum(picked, axis=1)


def rotary(projected, offsets, head_dim):
    token_count = projected.shape[0]
    heads_grid = projected.astype(jnp.float32).reshape(token_count, -1, head_dim)
    half_dim = head_dim // 2
    inverse = rope_theta ** (-2.0 * jnp.arange(half_dim).astype(jnp.float32) / head_dim)
    angles = offsets.astype(jnp.float32)[:, None] * inverse[None, :]
    cosine = jnp.cos(angles)[:, None, :]
    sine_part = jnp.sin(angles)[:, None, :]
    first_half = heads_grid[..., :half_dim]
    second_half = heads_grid[..., half_dim:]
    rotated = jnp.concatenate(
        [
            first_half * cosine - second_half * sine_part,
            second_half * cosine + first_half * sine_part,
        ],
        axis=-1,
    )
    return rotated.reshape(token_count, -1).astype(jnp.bfloat16)


def make_body(n_ctx, n_head, row):
    def on_device(queries, key_proj, value_proj, lengths, out_weight):
        tok_rows = queries.shape[0]
        kv_width = key_proj.shape[1]
        kv_local = kv_width // HD
        query_group = queries.shape[1] // kv_width
        back = -(-(MOST - 1) // tok_rows)
        rows_back = -(-back // row)
        span = rows_back * row
        ctx = lax.axis_index("ctx")
        first_row = ctx * tok_rows
        positions = first_row + jnp.arange(tok_rows, dtype=jnp.int32)
        starts = doc_starts(lengths, positions)
        offsets = positions - starts
        q_rot = rotary(queries, offsets, HD).reshape(tok_rows, kv_local, query_group, HD)
        k_rot = rotary(key_proj, offsets, HD)
        own = jnp.concatenate([k_rot, value_proj], axis=1)

        bundle = [own]
        for m in range(1, rows_back + 1):
            shift = row * m
            bundle.append(lax.ppermute(own, "ctx", [(s, s + shift) for s in range(n_ctx - shift)]))
        blocks = {row * m: bundle[m] for m in range(rows_back + 1)}
        bundle = jnp.stack(bundle)
        z = ctx % row
        n_rows = n_ctx // row
        for chain in relay_plan(row, rows_back):
            packet = bundle
            for step in chain:
                lo = pick(step["send"], z)
                packet = lax.ppermute(
                    lax.dynamic_slice_in_dim(packet, lo, step["width"], 0),
                    "ctx",
                    [(r * row + s, r * row + (s + step["dir"]) % row) for r in range(n_rows) for s in range(row)],
                )
                at = pick(step["take"], z)
                got = lax.dynamic_slice_in_dim(packet, at, len(step["blocks"]), 0)
                for i, blk in enumerate(step["blocks"]):
                    blocks[blk] = got[i]
        window = jnp.concatenate([blocks[span - k] for k in range(span + 1)], axis=0)
        key_count = window.shape[0]
        key_block = window[:, :kv_width].reshape(key_count, kv_local, HD)
        value_block = window[:, kv_width:].reshape(key_count, kv_local, HD)

        scores = jnp.einsum(
            "tkgd,nkd->kgtn", q_rot, key_block, preferred_element_type=jnp.float32
        ) / jnp.sqrt(jnp.float32(HD))
        key_pos = (ctx - span) * tok_rows + jnp.arange(key_count, dtype=jnp.int32)
        allowed = (key_pos[None, :] <= positions[:, None]) & (key_pos[None, :] >= starts[:, None])
        scores = jnp.where(allowed, scores, -1e30)
        row_max = jnp.max(scores, axis=-1)
        weights = jnp.where(allowed, jnp.exp(scores - row_max[..., None]), 0.0)
        row_sum = jnp.sum(weights, axis=-1)
        weighted = jnp.einsum(
            "kgtn,nkd->kgtd",
            weights.astype(jnp.bfloat16),
            value_block,
            preferred_element_type=jnp.float32,
        )
        normed = (weighted / row_sum[..., None]).astype(jnp.bfloat16)
        attended = jnp.transpose(normed, (2, 0, 1, 3)).reshape(tok_rows, kv_local * query_group * HD)

        feat = attended.shape[1]
        head = lax.axis_index("head")
        core = head % 2

        def project(piece, src):
            rows = lax.dynamic_slice_in_dim(out_weight, src * feat, feat, 0)
            return jnp.dot(piece, rows, preferred_element_type=jnp.float32)

        up = lax.ppermute(attended, "head", [(s, (s + 2) % n_head) for s in range(n_head)])
        down = lax.ppermute(attended, "head", [(s, (s - 2) % n_head) for s in range(n_head)])
        swap = [(s, s ^ 1) for s in range(n_head)]
        partner = lax.ppermute(attended, "head", swap)
        relay_pairs = [(s, (s + 2) % n_head) if s % 2 == 0 else (s, (s - 2) % n_head) for s in range(n_head)]
        far = lax.ppermute(jnp.where(core == 0, up, down), "head", relay_pairs)
        near_other = lax.ppermute(jnp.stack([up, down]), "head", swap)
        far_other = lax.ppermute(far, "head", swap)
        other = head ^ 1
        total = project(attended, head)
        total = total + project(up, (head - 2) % n_head)
        total = total + project(down, (head + 2) % n_head)
        total = total + project(partner, other)
        total = total + project(far, (head + 4) % n_head)
        total = total + project(near_other[0], (other - 2) % n_head)
        total = total + project(near_other[1], (other + 2) % n_head)
        total = total + project(far_other, (other + 4) % n_head)
        return total.astype(jnp.bfloat16)

    return on_device


def pick(table, z):
    out = jnp.int32(0)
    for i, v in enumerate(table):
        if v:
            out = out + jnp.where(z == i, jnp.int32(v), jnp.int32(0))
    return out


def relay_plan(row, rows_back):
    half = row // 2
    split = row % 2 == 0

    def part(z, b, direction):
        lo = 1 if z < b else 0
        slots = list(range(lo, lo + rows_back))
        if split and b == half:
            cut = (rows_back + 1) // 2
            slots = slots[:cut] if direction == 1 else slots[cut:]
        return slots

    chains = []
    for direction in (1, -1):
        rounds = range(1, half + 1) if direction == 1 else range(1, (half if split else row - 1 - half) + 1)
        bs = [r if direction == 1 else row - r for r in rounds]
        steps, held = [], None
        for i, b in enumerate(bs):
            need = {}
            for n in range(row):
                source = (n - direction * i) % row
                slots = set()
                for later in bs[i:]:
                    receiver = (source + later) % row
                    slots.update(part(receiver, later, direction))
                need[n] = slots
            width = max(max(v) - min(v) + 1 for v in need.values())
            lo = {n: min(min(v), rows_back + 1 - width) for n, v in need.items()}
            send = []
            for z in range(row):
                offset = lo[z] - (0 if held is None else held[(z - direction) % row])
                assert 0 <= offset and offset + width <= (rows_back + 1 if held is None else steps[-1]["width"])
                send.append(offset)
            take, blocks = [], None
            for z in range(row):
                sender = (z - direction) % row
                slots = part(z, b, direction)
                take.append(slots[0] - lo[sender])
                lo_z = 1 if z < b else 0
                mine = [b + row * (m - lo_z) for m in slots]
                assert blocks is None or blocks == mine
                blocks = mine
            steps.append({"dir": direction, "width": width, "send": send, "take": take, "blocks": blocks})
            held = lo
        chains.append(steps)
    return chains


def solution(mesh):
    n_ctx, n_head = mesh.shape["ctx"], mesh.shape["head"]
    row = 8 if n_ctx % 8 == 0 else n_ctx
    placed = (P("ctx", "head"), P("ctx", "head"), P("ctx", "head"), P(), P(None, "head"))
    return jax.shard_map(
        make_body(n_ctx, n_head, row), mesh=mesh, in_specs=placed, out_specs=P("ctx", "head"), check_vma=False
    )
```

```python
import jax
import jax.numpy as jnp
from jax import lax
from jax.sharding import PartitionSpec as P

HD = 128
MOST = 2048


rope_theta = 500000.0


def doc_starts(lengths, positions):
    doc_ends = jnp.cumsum(lengths)
    picked = jnp.where(doc_ends[None, :] <= positions[:, None], lengths[None, :], 0)
    return jnp.sum(picked, axis=1)


def rotary(projected, offsets, head_dim):
    token_count = projected.shape[0]
    heads_grid = projected.astype(jnp.float32).reshape(token_count, -1, head_dim)
    half_dim = head_dim // 2
    inverse = rope_theta ** (-2.0 * jnp.arange(half_dim).astype(jnp.float32) / head_dim)
    angles = offsets.astype(jnp.float32)[:, None] * inverse[None, :]
    cosine = jnp.cos(angles)[:, None, :]
    sine_part = jnp.sin(angles)[:, None, :]
    first_half = heads_grid[..., :half_dim]
    second_half = heads_grid[..., half_dim:]
    rotated = jnp.concatenate(
        [
            first_half * cosine - second_half * sine_part,
            second_half * cosine + first_half * sine_part,
        ],
        axis=-1,
    )
    return rotated.reshape(token_count, -1).astype(jnp.bfloat16)


def make_body(n_ctx, n_head, row):
    def on_device(queries, key_proj, value_proj, lengths, out_weight):
        tok_rows = queries.shape[0]
        kv_width = key_proj.shape[1]
        kv_local = kv_width // HD
        query_group = queries.shape[1] // kv_width
        back = -(-(MOST - 1) // tok_rows)
        rows_back = -(-back // row)
        span = rows_back * row
        ctx = lax.axis_index("ctx")
        first_row = ctx * tok_rows
        positions = first_row + jnp.arange(tok_rows, dtype=jnp.int32)
        starts = doc_starts(lengths, positions)
        offsets = positions - starts
        q_rot = rotary(queries, offsets, HD).reshape(tok_rows, kv_local, query_group, HD)
        k_rot = rotary(key_proj, offsets, HD)
        own = jnp.concatenate([k_rot, value_proj], axis=1)

        bundle = [own]
        for m in range(1, rows_back + 1):
            shift = row * m
            bundle.append(lax.ppermute(own, "ctx", [(s, s + shift) for s in range(n_ctx - shift)]))
        blocks = {row * m: bundle[m] for m in range(rows_back + 1)}
        bundle = jnp.stack(bundle)
        z = ctx % row
        n_rows = n_ctx // row
        chains, direct = relay_plan(row, rows_back)
        if direct:
            half = row // 2
            lo = jnp.where((z + half) % row < half, 1, 0)
            got = lax.ppermute(
                lax.dynamic_slice_in_dim(bundle, lo, rows_back, 0),
                "ctx",
                [(r * row + s, r * row + (s + half) % row) for r in range(n_rows) for s in range(row)],
            )
            for m in range(rows_back):
                blocks[half + row * m] = got[m]
        for chain in chains:
            packet = bundle
            for step in chain:
                lo = pick(step["send"], z)
                packet = lax.ppermute(
                    lax.dynamic_slice_in_dim(packet, lo, step["width"], 0),
                    "ctx",
                    [(r * row + s, r * row + (s + step["dir"]) % row) for r in range(n_rows) for s in range(row)],
                )
                at = pick(step["take"], z)
                got = lax.dynamic_slice_in_dim(packet, at, len(step["blocks"]), 0)
                for i, blk in enumerate(step["blocks"]):
                    blocks[blk] = got[i]
        window = jnp.concatenate([blocks[span - k] for k in range(span + 1)], axis=0)
        key_count = window.shape[0]
        key_block = window[:, :kv_width].reshape(key_count, kv_local, HD)
        value_block = window[:, kv_width:].reshape(key_count, kv_local, HD)

        scores = jnp.einsum(
            "tkgd,nkd->kgtn", q_rot, key_block, preferred_element_type=jnp.float32
        ) / jnp.sqrt(jnp.float32(HD))
        key_pos = (ctx - span) * tok_rows + jnp.arange(key_count, dtype=jnp.int32)
        allowed = (key_pos[None, :] <= positions[:, None]) & (key_pos[None, :] >= starts[:, None])
        scores = jnp.where(allowed, scores, -1e30)
        row_max = jnp.max(scores, axis=-1)
        weights = jnp.where(allowed, jnp.exp(scores - row_max[..., None]), 0.0)
        row_sum = jnp.sum(weights, axis=-1)
        weighted = jnp.einsum(
            "kgtn,nkd->kgtd",
            weights.astype(jnp.bfloat16),
            value_block,
            preferred_element_type=jnp.float32,
        )
        normed = (weighted / row_sum[..., None]).astype(jnp.bfloat16)
        attended = jnp.transpose(normed, (2, 0, 1, 3)).reshape(tok_rows, kv_local * query_group * HD)

        feat = attended.shape[1]
        head = lax.axis_index("head")
        core = head % 2

        def project(piece, src):
            rows = lax.dynamic_slice_in_dim(out_weight, src * feat, feat, 0)
            return jnp.dot(piece, rows, preferred_element_type=jnp.float32)

        up = lax.ppermute(attended, "head", [(s, (s + 2) % n_head) for s in range(n_head)])
        down = lax.ppermute(attended, "head", [(s, (s - 2) % n_head) for s in range(n_head)])
        swap = [(s, s ^ 1) for s in range(n_head)]
        partner = lax.ppermute(attended, "head", swap)
        relay_pairs = [(s, (s + 2) % n_head) if s % 2 == 0 else (s, (s - 2) % n_head) for s in range(n_head)]
        far = lax.ppermute(jnp.where(core == 0, up, down), "head", relay_pairs)
        near_other = lax.ppermute(jnp.stack([up, down]), "head", swap)
        far_other = lax.ppermute(far, "head", swap)
        other = head ^ 1
        total = project(attended, head)
        total = total + project(up, (head - 2) % n_head)
        total = total + project(down, (head + 2) % n_head)
        total = total + project(partner, other)
        total = total + project(far, (head + 4) % n_head)
        total = total + project(near_other[0], (other - 2) % n_head)
        total = total + project(near_other[1], (other + 2) % n_head)
        total = total + project(far_other, (other + 4) % n_head)
        return total.astype(jnp.bfloat16)

    return on_device


def pick(table, z):
    out = jnp.int32(0)
    for i, v in enumerate(table):
        if v:
            out = out + jnp.where(z == i, jnp.int32(v), jnp.int32(0))
    return out


def relay_plan(row, rows_back):
    half = row // 2
    direct = row % 2 == 0 and row > 2
    split = False

    def part(z, b, direction):
        lo = 1 if z < b else 0
        slots = list(range(lo, lo + rows_back))
        if split and b == half:
            cut = (rows_back + 1) // 2
            slots = slots[:cut] if direction == 1 else slots[cut:]
        return slots

    chains = []
    for direction in (1, -1):
        rounds = range(1, (half - 1 if direct else half) + 1) if direction == 1 else range(1, row - 1 - half + 1)
        bs = [r if direction == 1 else row - r for r in rounds]
        steps, held = [], None
        for i, b in enumerate(bs):
            need = {}
            for n in range(row):
                source = (n - direction * i) % row
                slots = set()
                for later in bs[i:]:
                    receiver = (source + later) % row
                    slots.update(part(receiver, later, direction))
                need[n] = slots
            width = max(max(v) - min(v) + 1 for v in need.values())
            lo = {n: min(min(v), rows_back + 1 - width) for n, v in need.items()}
            send = []
            for z in range(row):
                offset = lo[z] - (0 if held is None else held[(z - direction) % row])
                assert 0 <= offset and offset + width <= (rows_back + 1 if held is None else steps[-1]["width"])
                send.append(offset)
            take, blocks = [], None
            for z in range(row):
                sender = (z - direction) % row
                slots = part(z, b, direction)
                take.append(slots[0] - lo[sender])
                lo_z = 1 if z < b else 0
                mine = [b + row * (m - lo_z) for m in slots]
                assert blocks is None or blocks == mine
                blocks = mine
            steps.append({"dir": direction, "width": width, "send": send, "take": take, "blocks": blocks})
            held = lo
        chains.append(steps)
    return chains, direct


def solution(mesh):
    n_ctx, n_head = mesh.shape["ctx"], mesh.shape["head"]
    row = 8 if n_ctx % 8 == 0 else n_ctx
    placed = (P("ctx", "head"), P("ctx", "head"), P("ctx", "head"), P(), P(None, "head"))
    return jax.shard_map(
        make_body(n_ctx, n_head, row), mesh=mesh, in_specs=placed, out_specs=P("ctx", "head"), check_vma=False
    )
```

```python
import jax
import jax.numpy as jnp
from jax import lax
from jax.sharding import PartitionSpec as P

HD = 128
MOST = 2048


rope_theta = 500000.0


def doc_starts(lengths, positions):
    doc_ends = jnp.cumsum(lengths)
    picked = jnp.where(doc_ends[None, :] <= positions[:, None], lengths[None, :], 0)
    return jnp.sum(picked, axis=1)


def rotary(projected, offsets, head_dim):
    token_count = projected.shape[0]
    heads_grid = projected.astype(jnp.float32).reshape(token_count, -1, head_dim)
    half_dim = head_dim // 2
    inverse = rope_theta ** (-2.0 * jnp.arange(half_dim).astype(jnp.float32) / head_dim)
    angles = offsets.astype(jnp.float32)[:, None] * inverse[None, :]
    cosine = jnp.cos(angles)[:, None, :]
    sine_part = jnp.sin(angles)[:, None, :]
    first_half = heads_grid[..., :half_dim]
    second_half = heads_grid[..., half_dim:]
    rotated = jnp.concatenate(
        [
            first_half * cosine - second_half * sine_part,
            second_half * cosine + first_half * sine_part,
        ],
        axis=-1,
    )
    return rotated.reshape(token_count, -1).astype(jnp.bfloat16)


def make_body(n_ctx, n_head, row):
    def on_device(queries, key_proj, value_proj, lengths, out_weight):
        tok_rows = queries.shape[0]
        kv_width = key_proj.shape[1]
        kv_local = kv_width // HD
        query_group = queries.shape[1] // kv_width
        back = -(-(MOST - 1) // tok_rows)
        rows_back = -(-back // row)
        span = rows_back * row
        ctx = lax.axis_index("ctx")
        first_row = ctx * tok_rows
        positions = first_row + jnp.arange(tok_rows, dtype=jnp.int32)
        starts = doc_starts(lengths, positions)
        offsets = positions - starts
        q_rot = rotary(queries, offsets, HD).reshape(tok_rows, kv_local, query_group, HD)
        k_rot = rotary(key_proj, offsets, HD)
        own = jnp.concatenate([k_rot, value_proj], axis=1)

        bundle = [own]
        for m in range(1, rows_back + 1):
            shift = row * m
            bundle.append(lax.ppermute(own, "ctx", [(s, s + shift) for s in range(n_ctx - shift)]))
        blocks = {row * m: bundle[m] for m in range(rows_back + 1)}
        bundle = jnp.stack(bundle)
        z = ctx % row
        n_rows = n_ctx // row
        chains, direct = relay_plan(row, rows_back)
        if direct:
            half = row // 2
            lo = jnp.where((z + half) % row < half, 1, 0)
            got = lax.ppermute(
                lax.dynamic_slice_in_dim(bundle, lo, rows_back, 0),
                "ctx",
                [(r * row + s, r * row + (s + half) % row) for r in range(n_rows) for s in range(row)],
            )
            for m in range(rows_back):
                blocks[half + row * m] = got[m]
        for chain in chains:
            packet = bundle
            for step in chain:
                lo = pick(step["send"], z)
                packet = lax.ppermute(
                    lax.dynamic_slice_in_dim(packet, lo, step["width"], 0),
                    "ctx",
                    [(r * row + s, r * row + (s + step["dir"]) % row) for r in range(n_rows) for s in range(row)],
                )
                at = pick(step["take"], z)
                got = lax.dynamic_slice_in_dim(packet, at, len(step["blocks"]), 0)
                for i, blk in enumerate(step["blocks"]):
                    blocks[blk] = got[i]
        window = jnp.concatenate([blocks[span - k] for k in range(span + 1)], axis=0)
        key_count = window.shape[0]
        key_block = window[:, :kv_width].reshape(key_count, kv_local, HD)
        value_block = window[:, kv_width:].reshape(key_count, kv_local, HD)

        scores = jnp.einsum(
            "tkgd,nkd->kgtn", q_rot, key_block, preferred_element_type=jnp.float32
        ) / jnp.sqrt(jnp.float32(HD))
        key_pos = (ctx - span) * tok_rows + jnp.arange(key_count, dtype=jnp.int32)
        allowed = (key_pos[None, :] <= positions[:, None]) & (key_pos[None, :] >= starts[:, None])
        scores = jnp.where(allowed, scores, -1e30)
        row_max = jnp.max(scores, axis=-1)
        weights = jnp.where(allowed, jnp.exp(scores - row_max[..., None]), 0.0)
        row_sum = jnp.sum(weights, axis=-1)
        weighted = jnp.einsum(
            "kgtn,nkd->kgtd",
            weights.astype(jnp.bfloat16),
            value_block,
            preferred_element_type=jnp.float32,
        )
        normed = (weighted / row_sum[..., None]).astype(jnp.bfloat16)
        attended = jnp.transpose(normed, (2, 0, 1, 3)).reshape(tok_rows, kv_local * query_group * HD)

        feat = attended.shape[1]
        head = lax.axis_index("head")
        core = head % 2

        def project(piece, src):
            rows = lax.dynamic_slice_in_dim(out_weight, src * feat, feat, 0)
            return jnp.dot(piece, rows, preferred_element_type=jnp.float32)

        up = lax.ppermute(attended, "head", [(s, (s + 2) % n_head) for s in range(n_head)])
        down = lax.ppermute(attended, "head", [(s, (s - 2) % n_head) for s in range(n_head)])
        swap = [(s, s ^ 1) for s in range(n_head)]
        partner = lax.ppermute(attended, "head", swap)
        same_pairs = [(s, (s + 2) % n_head) if s % 2 == 0 else (s, (s - 2) % n_head) for s in range(n_head)]
        far = lax.ppermute(jnp.where(core == 0, up, down), "head", same_pairs)
        cross_pairs = [(s, (s + 1) % n_head) if s % 2 == 1 else (s, (s - 1) % n_head) for s in range(n_head)]
        far_cross = lax.ppermute(jnp.where(core == 1, up, down), "head", cross_pairs)
        near_other = lax.ppermute(jnp.stack([up, down]), "head", swap)
        other = head ^ 1
        total = project(attended, head)
        total = total + project(up, (head - 2) % n_head)
        total = total + project(down, (head + 2) % n_head)
        total = total + project(partner, other)
        total = total + project(far, (head + 4) % n_head)
        total = total + project(far_cross, jnp.where(core == 0, head - 3, head + 3) % n_head)
        total = total + project(near_other[0], (other - 2) % n_head)
        total = total + project(near_other[1], (other + 2) % n_head)
        return total.astype(jnp.bfloat16)

    return on_device


def pick(table, z):
    out = jnp.int32(0)
    for i, v in enumerate(table):
        if v:
            out = out + jnp.where(z == i, jnp.int32(v), jnp.int32(0))
    return out


def relay_plan(row, rows_back):
    half = row // 2
    direct = row % 2 == 0 and row > 2
    split = False

    def part(z, b, direction):
        lo = 1 if z < b else 0
        slots = list(range(lo, lo + rows_back))
        if split and b == half:
            cut = (rows_back + 1) // 2
            slots = slots[:cut] if direction == 1 else slots[cut:]
        return slots

    chains = []
    for direction in (1, -1):
        rounds = range(1, (half - 1 if direct else half) + 1) if direction == 1 else range(1, row - 1 - half + 1)
        bs = [r if direction == 1 else row - r for r in rounds]
        steps, held = [], None
        for i, b in enumerate(bs):
            need = {}
            for n in range(row):
                source = (n - direction * i) % row
                slots = set()
                for later in bs[i:]:
                    receiver = (source + later) % row
                    slots.update(part(receiver, later, direction))
                need[n] = slots
            width = max(max(v) - min(v) + 1 for v in need.values())
            lo = {n: min(min(v), rows_back + 1 - width) for n, v in need.items()}
            send = []
            for z in range(row):
                offset = lo[z] - (0 if held is None else held[(z - direction) % row])
                assert 0 <= offset and offset + width <= (rows_back + 1 if held is None else steps[-1]["width"])
                send.append(offset)
            take, blocks = [], None
            for z in range(row):
                sender = (z - direction) % row
                slots = part(z, b, direction)
                take.append(slots[0] - lo[sender])
                lo_z = 1 if z < b else 0
                mine = [b + row * (m - lo_z) for m in slots]
                assert blocks is None or blocks == mine
                blocks = mine
            steps.append({"dir": direction, "width": width, "send": send, "take": take, "blocks": blocks})
            held = lo
        chains.append(steps)
    return chains, direct


def solution(mesh):
    n_ctx, n_head = mesh.shape["ctx"], mesh.shape["head"]
    row = 8 if n_ctx % 8 == 0 else n_ctx
    placed = (P("ctx", "head"), P("ctx", "head"), P("ctx", "head"), P(), P(None, "head"))
    return jax.shard_map(
        make_body(n_ctx, n_head, row), mesh=mesh, in_specs=placed, out_specs=P("ctx", "head"), check_vma=False
    )
```

```python
import jax
import jax.numpy as jnp
from jax import lax
from jax.sharding import PartitionSpec as P

HD = 128
MOST = 2048


rope_theta = 500000.0


def doc_starts(lengths, positions):
    idx = jnp.arange(lengths.shape[0])
    doc_ends = jnp.sum(jnp.where(idx[None, :] <= idx[:, None], lengths[None, :], 0), axis=1)
    picked = jnp.where(doc_ends[None, :] <= positions[:, None], lengths[None, :], 0)
    return jnp.sum(picked, axis=1)


def rotary(projected, offsets, head_dim):
    token_count = projected.shape[0]
    heads_grid = projected.astype(jnp.float32).reshape(token_count, -1, head_dim)
    half_dim = head_dim // 2
    inverse = rope_theta ** (-2.0 * jnp.arange(half_dim).astype(jnp.float32) / head_dim)
    angles = offsets.astype(jnp.float32)[:, None] * inverse[None, :]
    cosine = jnp.cos(angles)[:, None, :]
    sine_part = jnp.sin(angles)[:, None, :]
    first_half = heads_grid[..., :half_dim]
    second_half = heads_grid[..., half_dim:]
    rotated = jnp.concatenate(
        [
            first_half * cosine - second_half * sine_part,
            second_half * cosine + first_half * sine_part,
        ],
        axis=-1,
    )
    return rotated.reshape(token_count, -1).astype(jnp.bfloat16)


def make_body(n_ctx, n_head, row):
    def on_device(queries, key_proj, value_proj, lengths, out_weight):
        tok_rows = queries.shape[0]
        kv_width = key_proj.shape[1]
        kv_local = kv_width // HD
        query_group = queries.shape[1] // kv_width
        back = -(-(MOST - 1) // tok_rows)
        rows_back = -(-back // row)
        span = rows_back * row
        ctx = lax.axis_index("ctx")
        first_row = ctx * tok_rows
        positions = first_row + jnp.arange(tok_rows, dtype=jnp.int32)
        starts = doc_starts(lengths, positions)
        offsets = positions - starts
        q_rot = rotary(queries, offsets, HD).reshape(tok_rows, kv_local, query_group, HD)
        k_rot = rotary(key_proj, offsets, HD)
        own = jnp.concatenate([k_rot, value_proj], axis=1)

        bundle = [own]
        for m in range(1, rows_back + 1):
            shift = row * m
            bundle.append(lax.ppermute(own, "ctx", [(s, s + shift) for s in range(n_ctx - shift)]))
        blocks = {row * m: bundle[m] for m in range(rows_back + 1)}
        bundle = jnp.stack(bundle)
        z = ctx % row
        n_rows = n_ctx // row
        chains, direct = relay_plan(row, rows_back)
        if direct:
            half = row // 2
            lo = jnp.where((z + half) % row < half, 1, 0)
            got = lax.ppermute(
                lax.dynamic_slice_in_dim(bundle, lo, rows_back, 0),
                "ctx",
                [(r * row + s, r * row + (s + half) % row) for r in range(n_rows) for s in range(row)],
            )
            for m in range(rows_back):
                blocks[half + row * m] = got[m]
        for chain in chains:
            packet = bundle
            for step in chain:
                lo = pick(step["send"], z)
                packet = lax.ppermute(
                    lax.dynamic_slice_in_dim(packet, lo, step["width"], 0),
                    "ctx",
                    [(r * row + s, r * row + (s + step["dir"]) % row) for r in range(n_rows) for s in range(row)],
                )
                at = pick(step["take"], z)
                got = lax.dynamic_slice_in_dim(packet, at, len(step["blocks"]), 0)
                for i, blk in enumerate(step["blocks"]):
                    blocks[blk] = got[i]
        window = jnp.concatenate([blocks[span - k] for k in range(span + 1)], axis=0)
        key_count = window.shape[0]
        key_block = window[:, :kv_width].reshape(key_count, kv_local, HD)
        value_block = window[:, kv_width:].reshape(key_count, kv_local, HD)

        scores = jnp.einsum(
            "tkgd,nkd->kgtn", q_rot, key_block, preferred_element_type=jnp.float32
        ) / jnp.sqrt(jnp.float32(HD))
        key_pos = (ctx - span) * tok_rows + jnp.arange(key_count, dtype=jnp.int32)
        allowed = (key_pos[None, :] <= positions[:, None]) & (key_pos[None, :] >= starts[:, None])
        scores = jnp.where(allowed, scores, -1e30)
        row_max = jnp.max(scores, axis=-1)
        weights = jnp.where(allowed, jnp.exp(scores - row_max[..., None]), 0.0)
        row_sum = jnp.sum(weights, axis=-1)
        weighted = jnp.einsum(
            "kgtn,nkd->kgtd",
            weights.astype(jnp.bfloat16),
            value_block,
            preferred_element_type=jnp.float32,
        )
        normed = (weighted / row_sum[..., None]).astype(jnp.bfloat16)
        attended = jnp.transpose(normed, (2, 0, 1, 3)).reshape(tok_rows, kv_local * query_group * HD)

        feat = attended.shape[1]
        head = lax.axis_index("head")
        core = head % 2

        def project(piece, src):
            rows = lax.dynamic_slice_in_dim(out_weight, src * feat, feat, 0)
            return jnp.dot(piece, rows, preferred_element_type=jnp.float32)

        up = lax.ppermute(attended, "head", [(s, (s + 2) % n_head) for s in range(n_head)])
        down = lax.ppermute(attended, "head", [(s, (s - 2) % n_head) for s in range(n_head)])
        swap = [(s, s ^ 1) for s in range(n_head)]
        partner = lax.ppermute(attended, "head", swap)
        same_pairs = [(s, (s + 2) % n_head) if s % 2 == 0 else (s, (s - 2) % n_head) for s in range(n_head)]
        far = lax.ppermute(jnp.where(core == 0, up, down), "head", same_pairs)
        cross_pairs = [(s, (s + 1) % n_head) if s % 2 == 1 else (s, (s - 1) % n_head) for s in range(n_head)]
        far_cross = lax.ppermute(jnp.where(core == 1, up, down), "head", cross_pairs)
        near_other = lax.ppermute(jnp.stack([up, down]), "head", swap)
        other = head ^ 1
        total = project(attended, head)
        total = total + project(up, (head - 2) % n_head)
        total = total + project(down, (head + 2) % n_head)
        total = total + project(partner, other)
        total = total + project(far, (head + 4) % n_head)
        total = total + project(far_cross, jnp.where(core == 0, head - 3, head + 3) % n_head)
        total = total + project(near_other[0], (other - 2) % n_head)
        total = total + project(near_other[1], (other + 2) % n_head)
        return total.astype(jnp.bfloat16)

    return on_device


def pick(table, z):
    out = jnp.int32(0)
    for i, v in enumerate(table):
        if v:
            out = out + jnp.where(z == i, jnp.int32(v), jnp.int32(0))
    return out


def relay_plan(row, rows_back):
    half = row // 2
    direct = row % 2 == 0 and row > 2
    split = False

    def part(z, b, direction):
        lo = 1 if z < b else 0
        slots = list(range(lo, lo + rows_back))
        if split and b == half:
            cut = (rows_back + 1) // 2
            slots = slots[:cut] if direction == 1 else slots[cut:]
        return slots

    chains = []
    for direction in (1, -1):
        rounds = range(1, (half - 1 if direct else half) + 1) if direction == 1 else range(1, row - 1 - half + 1)
        bs = [r if direction == 1 else row - r for r in rounds]
        steps, held = [], None
        for i, b in enumerate(bs):
            need = {}
            for n in range(row):
                source = (n - direction * i) % row
                slots = set()
                for later in bs[i:]:
                    receiver = (source + later) % row
                    slots.update(part(receiver, later, direction))
                need[n] = slots
            width = max(max(v) - min(v) + 1 for v in need.values())
            lo = {n: min(min(v), rows_back + 1 - width) for n, v in need.items()}
            send = []
            for z in range(row):
                offset = lo[z] - (0 if held is None else held[(z - direction) % row])
                assert 0 <= offset and offset + width <= (rows_back + 1 if held is None else steps[-1]["width"])
                send.append(offset)
            take, blocks = [], None
            for z in range(row):
                sender = (z - direction) % row
                slots = part(z, b, direction)
                take.append(slots[0] - lo[sender])
                lo_z = 1 if z < b else 0
                mine = [b + row * (m - lo_z) for m in slots]
                assert blocks is None or blocks == mine
                blocks = mine
            steps.append({"dir": direction, "width": width, "send": send, "take": take, "blocks": blocks})
            held = lo
        chains.append(steps)
    return chains, direct


def solution(mesh):
    n_ctx, n_head = mesh.shape["ctx"], mesh.shape["head"]
    row = 8 if n_ctx % 8 == 0 else n_ctx
    placed = (P("ctx", "head"), P("ctx", "head"), P("ctx", "head"), P(), P(None, "head"))
    return jax.shard_map(
        make_body(n_ctx, n_head, row), mesh=mesh, in_specs=placed, out_specs=P("ctx", "head"), check_vma=False
    )
```

```python
import jax
import jax.numpy as jnp
from jax import lax
from jax.sharding import PartitionSpec as P

HD = 128
MOST = 2048


rope_theta = 500000.0


def doc_starts(lengths, positions):
    idx = jnp.arange(lengths.shape[0])
    doc_ends = jnp.sum(jnp.where(idx[None, :] <= idx[:, None], lengths[None, :], 0), axis=1)
    picked = jnp.where(doc_ends[None, :] <= positions[:, None], lengths[None, :], 0)
    return jnp.sum(picked, axis=1)


def rotary(projected, offsets, head_dim):
    token_count = projected.shape[0]
    heads_grid = projected.astype(jnp.float32).reshape(token_count, -1, head_dim)
    half_dim = head_dim // 2
    inverse = rope_theta ** (-2.0 * jnp.arange(half_dim).astype(jnp.float32) / head_dim)
    angles = offsets.astype(jnp.float32)[:, None] * inverse[None, :]
    cosine = jnp.cos(angles)[:, None, :]
    sine_part = jnp.sin(angles)[:, None, :]
    first_half = heads_grid[..., :half_dim]
    second_half = heads_grid[..., half_dim:]
    rotated = jnp.concatenate(
        [
            first_half * cosine - second_half * sine_part,
            second_half * cosine + first_half * sine_part,
        ],
        axis=-1,
    )
    return rotated.reshape(token_count, -1).astype(jnp.bfloat16)


def make_body(n_ctx, n_head, row):
    def on_device(queries, key_proj, value_proj, lengths, out_weight):
        tok_rows = queries.shape[0]
        kv_width = key_proj.shape[1]
        kv_local = kv_width // HD
        query_group = queries.shape[1] // kv_width
        back = -(-(MOST - 1) // tok_rows)
        rows_back = -(-back // row)
        span = rows_back * row
        ctx = lax.axis_index("ctx")
        first_row = ctx * tok_rows
        positions = first_row + jnp.arange(tok_rows, dtype=jnp.int32)
        starts = doc_starts(lengths, positions)
        offsets = positions - starts
        q_rot = rotary(queries, offsets, HD).reshape(tok_rows, kv_local, query_group, HD)
        k_rot = rotary(key_proj, offsets, HD)
        own = jnp.stack([k_rot.T, value_proj], axis=0)

        bundle = [own]
        for m in range(1, rows_back + 1):
            shift = row * m
            bundle.append(lax.ppermute(own, "ctx", [(s, s + shift) for s in range(n_ctx - shift)]))
        blocks = {row * m: bundle[m] for m in range(rows_back + 1)}
        bundle = jnp.stack(bundle)
        z = ctx % row
        n_rows = n_ctx // row
        chains, direct = relay_plan(row, rows_back)
        if direct:
            half = row // 2
            lo = jnp.where((z + half) % row < half, 1, 0)
            got = lax.ppermute(
                lax.dynamic_slice_in_dim(bundle, lo, rows_back, 0),
                "ctx",
                [(r * row + s, r * row + (s + half) % row) for r in range(n_rows) for s in range(row)],
            )
            for m in range(rows_back):
                blocks[half + row * m] = got[m]
        for chain in chains:
            packet = bundle
            for step in chain:
                lo = pick(step["send"], z)
                packet = lax.ppermute(
                    lax.dynamic_slice_in_dim(packet, lo, step["width"], 0),
                    "ctx",
                    [(r * row + s, r * row + (s + step["dir"]) % row) for r in range(n_rows) for s in range(row)],
                )
                at = pick(step["take"], z)
                got = lax.dynamic_slice_in_dim(packet, at, len(step["blocks"]), 0)
                for i, blk in enumerate(step["blocks"]):
                    blocks[blk] = got[i]
        key_count = (span + 1) * tok_rows
        key_block = jnp.concatenate([blocks[span - k][0] for k in range(span + 1)], axis=1).T.reshape(key_count, kv_local, HD)
        value_block = jnp.concatenate([blocks[span - k][1] for k in range(span + 1)], axis=0).reshape(key_count, kv_local, HD)

        scores = jnp.einsum(
            "tkgd,nkd->kgtn", q_rot, key_block, preferred_element_type=jnp.float32
        ) / jnp.sqrt(jnp.float32(HD))
        key_pos = (ctx - span) * tok_rows + jnp.arange(key_count, dtype=jnp.int32)
        allowed = (key_pos[None, :] <= positions[:, None]) & (key_pos[None, :] >= starts[:, None])
        scores = jnp.where(allowed, scores, -1e30)
        row_max = jnp.max(scores, axis=-1)
        weights = jnp.where(allowed, jnp.exp(scores - row_max[..., None]), 0.0)
        row_sum = jnp.sum(weights, axis=-1)
        weighted = jnp.einsum(
            "kgtn,nkd->kgtd",
            weights.astype(jnp.bfloat16),
            value_block,
            preferred_element_type=jnp.float32,
        )
        normed = (weighted / row_sum[..., None]).astype(jnp.bfloat16)
        attended = jnp.transpose(normed, (2, 0, 1, 3)).reshape(tok_rows, kv_local * query_group * HD)

        feat = attended.shape[1]
        head = lax.axis_index("head")
        core = head % 2

        def project(piece, src):
            rows = lax.dynamic_slice_in_dim(out_weight, src * feat, feat, 0)
            return jnp.dot(piece, rows, preferred_element_type=jnp.float32)

        up = lax.ppermute(attended, "head", [(s, (s + 2) % n_head) for s in range(n_head)])
        down = lax.ppermute(attended, "head", [(s, (s - 2) % n_head) for s in range(n_head)])
        swap = [(s, s ^ 1) for s in range(n_head)]
        partner = lax.ppermute(attended, "head", swap)
        same_pairs = [(s, (s + 2) % n_head) if s % 2 == 0 else (s, (s - 2) % n_head) for s in range(n_head)]
        far = lax.ppermute(jnp.where(core == 0, up, down), "head", same_pairs)
        cross_pairs = [(s, (s + 1) % n_head) if s % 2 == 1 else (s, (s - 1) % n_head) for s in range(n_head)]
        far_cross = lax.ppermute(jnp.where(core == 1, up, down), "head", cross_pairs)
        near_other = lax.ppermute(jnp.stack([up, down]), "head", swap)
        other = head ^ 1
        total = project(attended, head)
        total = total + project(up, (head - 2) % n_head)
        total = total + project(down, (head + 2) % n_head)
        total = total + project(partner, other)
        total = total + project(far, (head + 4) % n_head)
        total = total + project(far_cross, jnp.where(core == 0, head - 3, head + 3) % n_head)
        total = total + project(near_other[0], (other - 2) % n_head)
        total = total + project(near_other[1], (other + 2) % n_head)
        return total.astype(jnp.bfloat16)

    return on_device


def pick(table, z):
    out = jnp.int32(0)
    for i, v in enumerate(table):
        if v:
            out = out + jnp.where(z == i, jnp.int32(v), jnp.int32(0))
    return out


def relay_plan(row, rows_back):
    half = row // 2
    direct = row % 2 == 0 and row > 2
    split = False

    def part(z, b, direction):
        lo = 1 if z < b else 0
        slots = list(range(lo, lo + rows_back))
        if split and b == half:
            cut = (rows_back + 1) // 2
            slots = slots[:cut] if direction == 1 else slots[cut:]
        return slots

    chains = []
    for direction in (1, -1):
        rounds = range(1, (half - 1 if direct else half) + 1) if direction == 1 else range(1, row - 1 - half + 1)
        bs = [r if direction == 1 else row - r for r in rounds]
        steps, held = [], None
        for i, b in enumerate(bs):
            need = {}
            for n in range(row):
                source = (n - direction * i) % row
                slots = set()
                for later in bs[i:]:
                    receiver = (source + later) % row
                    slots.update(part(receiver, later, direction))
                need[n] = slots
            width = max(max(v) - min(v) + 1 for v in need.values())
            lo = {n: min(min(v), rows_back + 1 - width) for n, v in need.items()}
            send = []
            for z in range(row):
                offset = lo[z] - (0 if held is None else held[(z - direction) % row])
                assert 0 <= offset and offset + width <= (rows_back + 1 if held is None else steps[-1]["width"])
                send.append(offset)
            take, blocks = [], None
            for z in range(row):
                sender = (z - direction) % row
                slots = part(z, b, direction)
                take.append(slots[0] - lo[sender])
                lo_z = 1 if z < b else 0
                mine = [b + row * (m - lo_z) for m in slots]
                assert blocks is None or blocks == mine
                blocks = mine
            steps.append({"dir": direction, "width": width, "send": send, "take": take, "blocks": blocks})
            held = lo
        chains.append(steps)
    return chains, direct


def solution(mesh):
    n_ctx, n_head = mesh.shape["ctx"], mesh.shape["head"]
    row = 8 if n_ctx % 8 == 0 else n_ctx
    placed = (P("ctx", "head"), P("ctx", "head"), P("ctx", "head"), P(), P(None, "head"))
    return jax.shard_map(
        make_body(n_ctx, n_head, row), mesh=mesh, in_specs=placed, out_specs=P("ctx", "head"), check_vma=False
    )
```

```python
import jax
import jax.numpy as jnp
from jax import lax
from jax.sharding import PartitionSpec as P

HD = 128
MOST = 2048


rope_theta = 500000.0


def doc_starts(lengths, positions):
    idx = jnp.arange(lengths.shape[0])
    doc_ends = jnp.sum(jnp.where(idx[None, :] <= idx[:, None], lengths[None, :], 0), axis=1)
    picked = jnp.where(doc_ends[None, :] <= positions[:, None], lengths[None, :], 0)
    return jnp.sum(picked, axis=1)


def rotary(projected, offsets, head_dim):
    token_count = projected.shape[0]
    heads_grid = projected.astype(jnp.float32).reshape(token_count, -1, head_dim)
    half_dim = head_dim // 2
    inverse = rope_theta ** (-2.0 * jnp.arange(half_dim).astype(jnp.float32) / head_dim)
    angles = offsets.astype(jnp.float32)[:, None] * inverse[None, :]
    cosine = jnp.cos(angles)[:, None, :]
    sine_part = jnp.sin(angles)[:, None, :]
    first_half = heads_grid[..., :half_dim]
    second_half = heads_grid[..., half_dim:]
    rotated = jnp.concatenate(
        [
            first_half * cosine - second_half * sine_part,
            second_half * cosine + first_half * sine_part,
        ],
        axis=-1,
    )
    return rotated.reshape(token_count, -1).astype(jnp.bfloat16)


def make_body(n_ctx, n_head, row):
    def on_device(queries, key_proj, value_proj, lengths, out_weight):
        tok_rows = queries.shape[0]
        kv_width = key_proj.shape[1]
        kv_local = kv_width // HD
        query_group = queries.shape[1] // kv_width
        back = -(-(MOST - 1) // tok_rows)
        rows_back = -(-back // row)
        span = rows_back * row
        ctx = lax.axis_index("ctx")
        first_row = ctx * tok_rows
        positions = first_row + jnp.arange(tok_rows, dtype=jnp.int32)
        starts = doc_starts(lengths, positions)
        offsets = positions - starts
        q_rot = rotary(queries, offsets, HD).reshape(tok_rows, kv_local, query_group, HD)
        k_rot = rotary(key_proj, offsets, HD)
        own = jnp.concatenate([k_rot, value_proj], axis=1)

        bundle = [own]
        for m in range(1, rows_back + 1):
            shift = row * m
            bundle.append(lax.ppermute(own, "ctx", [(s, s + shift) for s in range(n_ctx - shift)]))
        blocks = {row * m: bundle[m] for m in range(rows_back + 1)}
        bundle = jnp.stack(bundle)
        z = ctx % row
        n_rows = n_ctx // row
        chains, direct = relay_plan(row, rows_back)
        if direct:
            half = row // 2
            lo = jnp.where((z + half) % row < half, 1, 0)
            got = lax.ppermute(
                lax.dynamic_slice_in_dim(bundle, lo, rows_back, 0),
                "ctx",
                [(r * row + s, r * row + (s + half) % row) for r in range(n_rows) for s in range(row)],
            )
            for m in range(rows_back):
                blocks[half + row * m] = got[m]
        for chain in chains:
            packet = bundle
            for step in chain:
                lo = pick(step["send"], z)
                packet = lax.ppermute(
                    lax.dynamic_slice_in_dim(packet, lo, step["width"], 0),
                    "ctx",
                    [(r * row + s, r * row + (s + step["dir"]) % row) for r in range(n_rows) for s in range(row)],
                )
                at = pick(step["take"], z)
                got = lax.dynamic_slice_in_dim(packet, at, len(step["blocks"]), 0)
                for i, blk in enumerate(step["blocks"]):
                    blocks[blk] = got[i]
        window = jnp.concatenate([blocks[span - k] for k in range(span + 1)], axis=0)
        key_count = window.shape[0]
        key_block = window[:, :kv_width].reshape(key_count, kv_local, HD)
        value_block = window[:, kv_width:].reshape(key_count, kv_local, HD)

        scores = jnp.einsum(
            "tkgd,nkd->kgtn", q_rot, key_block, preferred_element_type=jnp.float32
        ) / jnp.sqrt(jnp.float32(HD))
        key_pos = (ctx - span) * tok_rows + jnp.arange(key_count, dtype=jnp.int32)
        allowed = (key_pos[None, :] <= positions[:, None]) & (key_pos[None, :] >= starts[:, None])
        scores = jnp.where(allowed, scores, -1e30)
        row_max = jnp.max(scores, axis=-1)
        weights = jnp.where(allowed, jnp.exp(scores - row_max[..., None]), 0.0)
        row_sum = jnp.sum(weights, axis=-1)
        weighted = jnp.einsum(
            "kgtn,nkd->kgtd",
            weights.astype(jnp.bfloat16),
            value_block,
            preferred_element_type=jnp.float32,
        )
        normed = (weighted / row_sum[..., None]).astype(jnp.bfloat16)
        attended = jnp.transpose(normed, (2, 0, 1, 3)).reshape(tok_rows, kv_local * query_group * HD)

        feat = attended.shape[1]
        head = lax.axis_index("head")
        core = head % 2

        def project(piece, src):
            rows = lax.dynamic_slice_in_dim(out_weight, src * feat, feat, 0)
            return jnp.dot(piece, rows, preferred_element_type=jnp.float32)

        def gather(odd, even):
            pairs = [(s, (s + (odd if s % 2 else even)) % n_head) for s in range(n_head)]
            return lax.ppermute(attended, "head", pairs)

        total = project(attended, head)
        for odd, even in ((-1, 1), (2, 2), (-2, -2), (1, 3), (-3, -1), (4, 4), (3, 5)):
            got = gather(odd, even)
            shift = jnp.where(core == (1 if odd % 2 else 0), even, odd) if odd % 2 else jnp.int32(odd)
            total = total + project(got, (head - shift) % n_head)
        return total.astype(jnp.bfloat16)

    return on_device


def pick(table, z):
    out = jnp.int32(0)
    for i, v in enumerate(table):
        if v:
            out = out + jnp.where(z == i, jnp.int32(v), jnp.int32(0))
    return out


def relay_plan(row, rows_back):
    half = row // 2
    direct = row % 2 == 0 and row > 2
    split = False

    def part(z, b, direction):
        lo = 1 if z < b else 0
        slots = list(range(lo, lo + rows_back))
        if split and b == half:
            cut = (rows_back + 1) // 2
            slots = slots[:cut] if direction == 1 else slots[cut:]
        return slots

    chains = []
    for direction in (1, -1):
        rounds = range(1, (half - 1 if direct else half) + 1) if direction == 1 else range(1, row - 1 - half + 1)
        bs = [r if direction == 1 else row - r for r in rounds]
        steps, held = [], None
        for i, b in enumerate(bs):
            need = {}
            for n in range(row):
                source = (n - direction * i) % row
                slots = set()
                for later in bs[i:]:
                    receiver = (source + later) % row
                    slots.update(part(receiver, later, direction))
                need[n] = slots
            width = max(max(v) - min(v) + 1 for v in need.values())
            lo = {n: min(min(v), rows_back + 1 - width) for n, v in need.items()}
            send = []
            for z in range(row):
                offset = lo[z] - (0 if held is None else held[(z - direction) % row])
                assert 0 <= offset and offset + width <= (rows_back + 1 if held is None else steps[-1]["width"])
                send.append(offset)
            take, blocks = [], None
            for z in range(row):
                sender = (z - direction) % row
                slots = part(z, b, direction)
                take.append(slots[0] - lo[sender])
                lo_z = 1 if z < b else 0
                mine = [b + row * (m - lo_z) for m in slots]
                assert blocks is None or blocks == mine
                blocks = mine
            steps.append({"dir": direction, "width": width, "send": send, "take": take, "blocks": blocks})
            held = lo
        chains.append(steps)
    return chains, direct


def solution(mesh):
    n_ctx, n_head = mesh.shape["ctx"], mesh.shape["head"]
    row = 8 if n_ctx % 8 == 0 else n_ctx
    placed = (P("ctx", "head"), P("ctx", "head"), P("ctx", "head"), P(), P(None, "head"))
    return jax.shard_map(
        make_body(n_ctx, n_head, row), mesh=mesh, in_specs=placed, out_specs=P("ctx", "head"), check_vma=False
    )
```

```python
import jax
import jax.numpy as jnp
from jax import lax
from jax.sharding import PartitionSpec as P

HD = 128
MOST = 2048


rope_theta = 500000.0


def doc_starts(lengths, positions):
    idx = jnp.arange(lengths.shape[0])
    doc_ends = jnp.sum(jnp.where(idx[None, :] <= idx[:, None], lengths[None, :], 0), axis=1)
    picked = jnp.where(doc_ends[None, :] <= positions[:, None], lengths[None, :], 0)
    return jnp.sum(picked, axis=1)


def rotary(projected, offsets, head_dim):
    token_count = projected.shape[0]
    heads_grid = projected.astype(jnp.float32).reshape(token_count, -1, head_dim)
    half_dim = head_dim // 2
    inverse = rope_theta ** (-2.0 * jnp.arange(half_dim).astype(jnp.float32) / head_dim)
    angles = offsets.astype(jnp.float32)[:, None] * inverse[None, :]
    cosine = jnp.cos(angles)[:, None, :]
    sine_part = jnp.sin(angles)[:, None, :]
    first_half = heads_grid[..., :half_dim]
    second_half = heads_grid[..., half_dim:]
    rotated = jnp.concatenate(
        [
            first_half * cosine - second_half * sine_part,
            second_half * cosine + first_half * sine_part,
        ],
        axis=-1,
    )
    return rotated.reshape(token_count, -1).astype(jnp.bfloat16)


def make_body(n_ctx, n_head, row):
    def on_device(queries, key_proj, value_proj, lengths, out_weight):
        tok_rows = queries.shape[0]
        kv_width = key_proj.shape[1]
        kv_local = kv_width // HD
        query_group = queries.shape[1] // kv_width
        back = -(-(MOST - 1) // tok_rows)
        rows_back = -(-back // row)
        span = rows_back * row
        ctx = lax.axis_index("ctx")
        first_row = ctx * tok_rows
        positions = first_row + jnp.arange(tok_rows, dtype=jnp.int32)
        starts = doc_starts(lengths, positions)
        offsets = positions - starts
        q_rot = rotary(queries, offsets, HD).reshape(tok_rows, kv_local, query_group, HD)
        k_rot = rotary(key_proj, offsets, HD)
        own = jnp.concatenate([k_rot, value_proj], axis=1)

        bundle = [own]
        for m in range(1, rows_back + 1):
            shift = row * m
            bundle.append(lax.ppermute(own, "ctx", [(s, s + shift) for s in range(n_ctx - shift)]))
        blocks = {row * m: bundle[m] for m in range(rows_back + 1)}
        bundle = jnp.stack(bundle)
        z = ctx % row
        n_rows = n_ctx // row
        chains, direct = relay_plan(row, rows_back)
        if direct:
            half = row // 2
            lo = jnp.where((z + half) % row < half, 1, 0)
            got = lax.ppermute(
                lax.dynamic_slice_in_dim(bundle, lo, rows_back, 0),
                "ctx",
                [(r * row + s, r * row + (s + half) % row) for r in range(n_rows) for s in range(row)],
            )
            for m in range(rows_back):
                blocks[half + row * m] = got[m]
        for chain in chains:
            packet = bundle
            for step in chain:
                lo = pick(step["send"], z)
                packet = lax.ppermute(
                    lax.dynamic_slice_in_dim(packet, lo, step["width"], 0),
                    "ctx",
                    [(r * row + s, r * row + (s + step["dir"]) % row) for r in range(n_rows) for s in range(row)],
                )
                at = pick(step["take"], z)
                got = lax.dynamic_slice_in_dim(packet, at, len(step["blocks"]), 0)
                for i, blk in enumerate(step["blocks"]):
                    blocks[blk] = got[i]
        window = jnp.concatenate([blocks[span - k] for k in range(span + 1)], axis=0)
        key_count = window.shape[0]
        key_block = window[:, :kv_width].reshape(key_count, kv_local, HD)
        value_block = window[:, kv_width:].reshape(key_count, kv_local, HD)

        scores = jnp.einsum(
            "tkgd,nkd->kgtn", q_rot, key_block, preferred_element_type=jnp.float32
        ) / jnp.sqrt(jnp.float32(HD))
        key_pos = (ctx - span) * tok_rows + jnp.arange(key_count, dtype=jnp.int32)
        allowed = (key_pos[None, :] <= positions[:, None]) & (key_pos[None, :] >= starts[:, None])
        scores = jnp.where(allowed, scores, -1e30)
        row_max = jnp.max(scores, axis=-1)
        weights = jnp.where(allowed, jnp.exp(scores - row_max[..., None]), 0.0)
        row_sum = jnp.sum(weights, axis=-1)
        weighted = jnp.einsum(
            "kgtn,nkd->kgtd",
            weights.astype(jnp.bfloat16),
            value_block,
            preferred_element_type=jnp.float32,
        )
        normed = (weighted / row_sum[..., None]).astype(jnp.bfloat16)
        attended = jnp.transpose(normed, (2, 0, 1, 3)).reshape(tok_rows, kv_local * query_group * HD)

        feat = attended.shape[1]
        head = lax.axis_index("head")
        core = head % 2
        chip = head // 2
        n_chip = n_head // 2

        def project(pair, at):
            rows = lax.dynamic_slice_in_dim(out_weight, (at % n_chip) * 2 * feat, 2 * feat, 0)
            return jnp.dot(pair, rows, preferred_element_type=jnp.float32)

        partner = lax.ppermute(attended, "head", [(s, s ^ 1) for s in range(n_head)])
        pair = jnp.where(
            core == 0,
            jnp.concatenate([attended, partner], axis=1),
            jnp.concatenate([partner, attended], axis=1),
        )
        up = lax.ppermute(pair, "head", [(s, (s + 2) % n_head) for s in range(n_head)])
        down = lax.ppermute(pair, "head", [(s, (s - 2) % n_head) for s in range(n_head)])
        same_pairs = [(s, (s + 2) % n_head) if s % 2 == 0 else (s, (s - 2) % n_head) for s in range(n_head)]
        far = lax.ppermute(jnp.where(core == 0, up, down), "head", same_pairs)
        total = project(pair, chip)
        total = total + project(up, chip - 1)
        total = total + project(down, chip + 1)
        total = total + project(far, chip + 2)
        return total.astype(jnp.bfloat16)

    return on_device


def pick(table, z):
    out = jnp.int32(0)
    for i, v in enumerate(table):
        if v:
            out = out + jnp.where(z == i, jnp.int32(v), jnp.int32(0))
    return out


def relay_plan(row, rows_back):
    half = row // 2
    direct = row % 2 == 0 and row > 2
    split = False

    def part(z, b, direction):
        lo = 1 if z < b else 0
        slots = list(range(lo, lo + rows_back))
        if split and b == half:
            cut = (rows_back + 1) // 2
            slots = slots[:cut] if direction == 1 else slots[cut:]
        return slots

    chains = []
    for direction in (1, -1):
        rounds = range(1, (half - 1 if direct else half) + 1) if direction == 1 else range(1, row - 1 - half + 1)
        bs = [r if direction == 1 else row - r for r in rounds]
        steps, held = [], None
        for i, b in enumerate(bs):
            need = {}
            for n in range(row):
                source = (n - direction * i) % row
                slots = set()
                for later in bs[i:]:
                    receiver = (source + later) % row
                    slots.update(part(receiver, later, direction))
                need[n] = slots
            width = max(max(v) - min(v) + 1 for v in need.values())
            lo = {n: min(min(v), rows_back + 1 - width) for n, v in need.items()}
            send = []
            for z in range(row):
                offset = lo[z] - (0 if held is None else held[(z - direction) % row])
                assert 0 <= offset and offset + width <= (rows_back + 1 if held is None else steps[-1]["width"])
                send.append(offset)
            take, blocks = [], None
            for z in range(row):
                sender = (z - direction) % row
                slots = part(z, b, direction)
                take.append(slots[0] - lo[sender])
                lo_z = 1 if z < b else 0
                mine = [b + row * (m - lo_z) for m in slots]
                assert blocks is None or blocks == mine
                blocks = mine
            steps.append({"dir": direction, "width": width, "send": send, "take": take, "blocks": blocks})
            held = lo
        chains.append(steps)
    return chains, direct


def solution(mesh):
    n_ctx, n_head = mesh.shape["ctx"], mesh.shape["head"]
    row = 8 if n_ctx % 8 == 0 else n_ctx
    placed = (P("ctx", "head"), P("ctx", "head"), P("ctx", "head"), P(), P(None, "head"))
    return jax.shard_map(
        make_body(n_ctx, n_head, row), mesh=mesh, in_specs=placed, out_specs=P("ctx", "head"), check_vma=False
    )
```

```python
import jax
import jax.numpy as jnp
from jax import lax
from jax.sharding import PartitionSpec as P

HD = 128
MOST = 2048


rope_theta = 500000.0


def doc_starts(lengths, positions):
    idx = jnp.arange(lengths.shape[0])
    doc_ends = jnp.sum(jnp.where(idx[None, :] <= idx[:, None], lengths[None, :], 0), axis=1)
    picked = jnp.where(doc_ends[None, :] <= positions[:, None], lengths[None, :], 0)
    return jnp.sum(picked, axis=1)


def rotary(projected, offsets, head_dim):
    token_count = projected.shape[0]
    heads_grid = projected.astype(jnp.float32).reshape(token_count, -1, head_dim)
    half_dim = head_dim // 2
    inverse = rope_theta ** (-2.0 * jnp.arange(half_dim).astype(jnp.float32) / head_dim)
    angles = offsets.astype(jnp.float32)[:, None] * inverse[None, :]
    cosine = jnp.cos(angles)[:, None, :]
    sine_part = jnp.sin(angles)[:, None, :]
    first_half = heads_grid[..., :half_dim]
    second_half = heads_grid[..., half_dim:]
    rotated = jnp.concatenate(
        [
            first_half * cosine - second_half * sine_part,
            second_half * cosine + first_half * sine_part,
        ],
        axis=-1,
    )
    return rotated.reshape(token_count, -1).astype(jnp.bfloat16)


def make_body(n_ctx, n_head, row):
    def on_device(queries, key_proj, value_proj, lengths, out_weight):
        tok_rows = queries.shape[0]
        kv_width = key_proj.shape[1]
        kv_local = kv_width // HD
        query_group = queries.shape[1] // kv_width
        back = -(-(MOST - 1) // tok_rows)
        rows_back = -(-back // row)
        span = rows_back * row
        ctx = lax.axis_index("ctx")
        first_row = ctx * tok_rows
        positions = first_row + jnp.arange(tok_rows, dtype=jnp.int32)
        starts = doc_starts(lengths, positions)
        offsets = positions - starts
        q_rot = rotary(queries, offsets, HD).reshape(tok_rows, kv_local, query_group, HD)
        k_rot = rotary(key_proj, offsets, HD)
        own = jnp.concatenate([k_rot, value_proj], axis=1)

        bundle = [own]
        for m in range(1, rows_back + 1):
            shift = row * m
            bundle.append(lax.ppermute(own, "ctx", [(s, s + shift) for s in range(n_ctx - shift)]))
        blocks = {row * m: bundle[m] for m in range(rows_back + 1)}
        bundle = jnp.stack(bundle)
        z = ctx % row
        n_rows = n_ctx // row
        chains, direct = relay_plan(row, rows_back)
        first_round = []
        for chain in chains:
            packet = bundle
            for step in chain:
                lo = pick(step["send"], z)
                packet = lax.ppermute(
                    lax.dynamic_slice_in_dim(packet, lo, step["width"], 0),
                    "ctx",
                    [(r * row + s, r * row + (s + step["dir"]) % row) for r in range(n_rows) for s in range(row)],
                )
                if not first_round:
                    first_round.append(packet)
                at = pick(step["take"], z)
                got = lax.dynamic_slice_in_dim(packet, at, len(step["blocks"]), 0)
                for i, blk in enumerate(step["blocks"]):
                    blocks[blk] = got[i]
        if direct:
            half = row // 2
            lo = jnp.where((z + half) % row < half, 1, 0)
            payload, _ = lax.optimization_barrier((lax.dynamic_slice_in_dim(bundle, lo, rows_back, 0), first_round[0]))
            got = lax.ppermute(
                payload,
                "ctx",
                [(r * row + s, r * row + (s + half) % row) for r in range(n_rows) for s in range(row)],
            )
            for m in range(rows_back):
                blocks[half + row * m] = got[m]
        window = jnp.concatenate([blocks[span - k] for k in range(span + 1)], axis=0)
        key_count = window.shape[0]
        key_block = window[:, :kv_width].reshape(key_count, kv_local, HD)
        value_block = window[:, kv_width:].reshape(key_count, kv_local, HD)

        scores = jnp.einsum(
            "tkgd,nkd->kgtn", q_rot, key_block, preferred_element_type=jnp.float32
        ) / jnp.sqrt(jnp.float32(HD))
        key_pos = (ctx - span) * tok_rows + jnp.arange(key_count, dtype=jnp.int32)
        allowed = (key_pos[None, :] <= positions[:, None]) & (key_pos[None, :] >= starts[:, None])
        scores = jnp.where(allowed, scores, -1e30)
        row_max = jnp.max(scores, axis=-1)
        weights = jnp.where(allowed, jnp.exp(scores - row_max[..., None]), 0.0)
        row_sum = jnp.sum(weights, axis=-1)
        weighted = jnp.einsum(
            "kgtn,nkd->kgtd",
            weights.astype(jnp.bfloat16),
            value_block,
            preferred_element_type=jnp.float32,
        )
        normed = (weighted / row_sum[..., None]).astype(jnp.bfloat16)
        attended = jnp.transpose(normed, (2, 0, 1, 3)).reshape(tok_rows, kv_local * query_group * HD)

        feat = attended.shape[1]
        head = lax.axis_index("head")
        core = head % 2

        def project(piece, src):
            rows = lax.dynamic_slice_in_dim(out_weight, src * feat, feat, 0)
            return jnp.dot(piece, rows, preferred_element_type=jnp.float32)

        up = lax.ppermute(attended, "head", [(s, (s + 2) % n_head) for s in range(n_head)])
        down = lax.ppermute(attended, "head", [(s, (s - 2) % n_head) for s in range(n_head)])
        swap = [(s, s ^ 1) for s in range(n_head)]
        partner = lax.ppermute(attended, "head", swap)
        same_pairs = [(s, (s + 2) % n_head) if s % 2 == 0 else (s, (s - 2) % n_head) for s in range(n_head)]
        far = lax.ppermute(jnp.where(core == 0, up, down), "head", same_pairs)
        cross_pairs = [(s, (s + 1) % n_head) if s % 2 == 1 else (s, (s - 1) % n_head) for s in range(n_head)]
        far_cross = lax.ppermute(jnp.where(core == 1, up, down), "head", cross_pairs)
        near_other = lax.ppermute(jnp.stack([up, down]), "head", swap)
        other = head ^ 1
        total = project(attended, head)
        total = total + project(up, (head - 2) % n_head)
        total = total + project(down, (head + 2) % n_head)
        total = total + project(partner, other)
        total = total + project(far, (head + 4) % n_head)
        total = total + project(far_cross, jnp.where(core == 0, head - 3, head + 3) % n_head)
        total = total + project(near_other[0], (other - 2) % n_head)
        total = total + project(near_other[1], (other + 2) % n_head)
        return total.astype(jnp.bfloat16)

    return on_device


def pick(table, z):
    out = jnp.int32(0)
    for i, v in enumerate(table):
        if v:
            out = out + jnp.where(z == i, jnp.int32(v), jnp.int32(0))
    return out


def relay_plan(row, rows_back):
    half = row // 2
    direct = row % 2 == 0 and row > 2
    split = False

    def part(z, b, direction):
        lo = 1 if z < b else 0
        slots = list(range(lo, lo + rows_back))
        if split and b == half:
            cut = (rows_back + 1) // 2
            slots = slots[:cut] if direction == 1 else slots[cut:]
        return slots

    chains = []
    for direction in (1, -1):
        rounds = range(1, (half - 1 if direct else half) + 1) if direction == 1 else range(1, row - 1 - half + 1)
        bs = [r if direction == 1 else row - r for r in rounds]
        steps, held = [], None
        for i, b in enumerate(bs):
            need = {}
            for n in range(row):
                source = (n - direction * i) % row
                slots = set()
                for later in bs[i:]:
                    receiver = (source + later) % row
                    slots.update(part(receiver, later, direction))
                need[n] = slots
            width = max(max(v) - min(v) + 1 for v in need.values())
            lo = {n: min(min(v), rows_back + 1 - width) for n, v in need.items()}
            send = []
            for z in range(row):
                offset = lo[z] - (0 if held is None else held[(z - direction) % row])
                assert 0 <= offset and offset + width <= (rows_back + 1 if held is None else steps[-1]["width"])
                send.append(offset)
            take, blocks = [], None
            for z in range(row):
                sender = (z - direction) % row
                slots = part(z, b, direction)
                take.append(slots[0] - lo[sender])
                lo_z = 1 if z < b else 0
                mine = [b + row * (m - lo_z) for m in slots]
                assert blocks is None or blocks == mine
                blocks = mine
            steps.append({"dir": direction, "width": width, "send": send, "take": take, "blocks": blocks})
            held = lo
        chains.append(steps)
    return chains, direct


def solution(mesh):
    n_ctx, n_head = mesh.shape["ctx"], mesh.shape["head"]
    row = 8 if n_ctx % 8 == 0 else n_ctx
    placed = (P("ctx", "head"), P("ctx", "head"), P("ctx", "head"), P(), P(None, "head"))
    return jax.shard_map(
        make_body(n_ctx, n_head, row), mesh=mesh, in_specs=placed, out_specs=P("ctx", "head"), check_vma=False
    )
```

```python
import jax
import jax.numpy as jnp
from jax import lax
from jax.sharding import PartitionSpec as P

HD = 128
MOST = 2048


rope_theta = 500000.0


def doc_starts(lengths, positions):
    idx = jnp.arange(lengths.shape[0])
    doc_ends = jnp.sum(jnp.where(idx[None, :] <= idx[:, None], lengths[None, :], 0), axis=1)
    picked = jnp.where(doc_ends[None, :] <= positions[:, None], lengths[None, :], 0)
    return jnp.sum(picked, axis=1)


def rotary(projected, offsets, head_dim):
    token_count = projected.shape[0]
    heads_grid = projected.astype(jnp.float32).reshape(token_count, -1, head_dim)
    half_dim = head_dim // 2
    inverse = rope_theta ** (-2.0 * jnp.arange(half_dim).astype(jnp.float32) / head_dim)
    angles = offsets.astype(jnp.float32)[:, None] * inverse[None, :]
    cosine = jnp.cos(angles)[:, None, :]
    sine_part = jnp.sin(angles)[:, None, :]
    first_half = heads_grid[..., :half_dim]
    second_half = heads_grid[..., half_dim:]
    rotated = jnp.concatenate(
        [
            first_half * cosine - second_half * sine_part,
            second_half * cosine + first_half * sine_part,
        ],
        axis=-1,
    )
    return rotated.reshape(token_count, -1).astype(jnp.bfloat16)


def make_body(n_ctx, n_head, row):
    def on_device(queries, key_proj, value_proj, lengths, out_weight):
        tok_rows = queries.shape[0]
        kv_width = key_proj.shape[1]
        kv_local = kv_width // HD
        query_group = queries.shape[1] // kv_width
        back = -(-(MOST - 1) // tok_rows)
        rows_back = -(-back // row)
        span = rows_back * row
        ctx = lax.axis_index("ctx")
        raw = jnp.concatenate([key_proj, value_proj], axis=1)
        raw, lengths = lax.optimization_barrier((raw, lengths))
        first_row = ctx * tok_rows
        positions = first_row + jnp.arange(tok_rows, dtype=jnp.int32)
        starts = doc_starts(lengths, positions)
        offsets = positions - starts
        q_rot = rotary(queries, offsets, HD).reshape(tok_rows, kv_local, query_group, HD)
        own = jnp.concatenate([rotary(key_proj, offsets, HD), value_proj], axis=1)

        bundle = [own]
        for m in range(1, rows_back + 1):
            shift = row * m
            got = lax.ppermute(raw, "ctx", [(s, s + shift) for s in range(n_ctx - shift)])
            pos = (ctx - shift) * tok_rows + jnp.arange(tok_rows, dtype=jnp.int32)
            k_rot = rotary(got[:, :kv_width], pos - doc_starts(lengths, pos), HD)
            bundle.append(jnp.concatenate([k_rot, got[:, kv_width:]], axis=1))
        blocks = {row * m: bundle[m] for m in range(rows_back + 1)}
        bundle = jnp.stack(bundle)
        z = ctx % row
        n_rows = n_ctx // row
        chains, direct = relay_plan(row, rows_back)
        if direct:
            half = row // 2
            lo = jnp.where((z + half) % row < half, 1, 0)
            got = lax.ppermute(
                lax.dynamic_slice_in_dim(bundle, lo, rows_back, 0),
                "ctx",
                [(r * row + s, r * row + (s + half) % row) for r in range(n_rows) for s in range(row)],
            )
            for m in range(rows_back):
                blocks[half + row * m] = got[m]
        for chain in chains:
            packet = bundle
            for step in chain:
                lo = pick(step["send"], z)
                packet = lax.ppermute(
                    lax.dynamic_slice_in_dim(packet, lo, step["width"], 0),
                    "ctx",
                    [(r * row + s, r * row + (s + step["dir"]) % row) for r in range(n_rows) for s in range(row)],
                )
                at = pick(step["take"], z)
                got = lax.dynamic_slice_in_dim(packet, at, len(step["blocks"]), 0)
                for i, blk in enumerate(step["blocks"]):
                    blocks[blk] = got[i]
        window = jnp.concatenate([blocks[span - k] for k in range(span + 1)], axis=0)
        key_count = window.shape[0]
        key_block = window[:, :kv_width].reshape(key_count, kv_local, HD)
        value_block = window[:, kv_width:].reshape(key_count, kv_local, HD)

        scores = jnp.einsum(
            "tkgd,nkd->kgtn", q_rot, key_block, preferred_element_type=jnp.float32
        ) / jnp.sqrt(jnp.float32(HD))
        key_pos = (ctx - span) * tok_rows + jnp.arange(key_count, dtype=jnp.int32)
        allowed = (key_pos[None, :] <= positions[:, None]) & (key_pos[None, :] >= starts[:, None])
        scores = jnp.where(allowed, scores, -1e30)
        row_max = jnp.max(scores, axis=-1)
        weights = jnp.where(allowed, jnp.exp(scores - row_max[..., None]), 0.0)
        row_sum = jnp.sum(weights, axis=-1)
        weighted = jnp.einsum(
            "kgtn,nkd->kgtd",
            weights.astype(jnp.bfloat16),
            value_block,
            preferred_element_type=jnp.float32,
        )
        normed = (weighted / row_sum[..., None]).astype(jnp.bfloat16)
        attended = jnp.transpose(normed, (2, 0, 1, 3)).reshape(tok_rows, kv_local * query_group * HD)

        feat = attended.shape[1]
        head = lax.axis_index("head")
        core = head % 2

        def project(piece, src):
            rows = lax.dynamic_slice_in_dim(out_weight, src * feat, feat, 0)
            return jnp.dot(piece, rows, preferred_element_type=jnp.float32)

        up = lax.ppermute(attended, "head", [(s, (s + 2) % n_head) for s in range(n_head)])
        down = lax.ppermute(attended, "head", [(s, (s - 2) % n_head) for s in range(n_head)])
        swap = [(s, s ^ 1) for s in range(n_head)]
        partner = lax.ppermute(attended, "head", swap)
        same_pairs = [(s, (s + 2) % n_head) if s % 2 == 0 else (s, (s - 2) % n_head) for s in range(n_head)]
        far = lax.ppermute(jnp.where(core == 0, up, down), "head", same_pairs)
        cross_pairs = [(s, (s + 1) % n_head) if s % 2 == 1 else (s, (s - 1) % n_head) for s in range(n_head)]
        far_cross = lax.ppermute(jnp.where(core == 1, up, down), "head", cross_pairs)
        near_other = lax.ppermute(jnp.stack([up, down]), "head", swap)
        other = head ^ 1
        total = project(attended, head)
        total = total + project(up, (head - 2) % n_head)
        total = total + project(down, (head + 2) % n_head)
        total = total + project(partner, other)
        total = total + project(far, (head + 4) % n_head)
        total = total + project(far_cross, jnp.where(core == 0, head - 3, head + 3) % n_head)
        total = total + project(near_other[0], (other - 2) % n_head)
        total = total + project(near_other[1], (other + 2) % n_head)
        return total.astype(jnp.bfloat16)

    return on_device


def pick(table, z):
    out = jnp.int32(0)
    for i, v in enumerate(table):
        if v:
            out = out + jnp.where(z == i, jnp.int32(v), jnp.int32(0))
    return out


def relay_plan(row, rows_back):
    half = row // 2
    direct = row % 2 == 0 and row > 2
    split = False

    def part(z, b, direction):
        lo = 1 if z < b else 0
        slots = list(range(lo, lo + rows_back))
        if split and b == half:
            cut = (rows_back + 1) // 2
            slots = slots[:cut] if direction == 1 else slots[cut:]
        return slots

    chains = []
    for direction in (1, -1):
        rounds = range(1, (half - 1 if direct else half) + 1) if direction == 1 else range(1, row - 1 - half + 1)
        bs = [r if direction == 1 else row - r for r in rounds]
        steps, held = [], None
        for i, b in enumerate(bs):
            need = {}
            for n in range(row):
                source = (n - direction * i) % row
                slots = set()
                for later in bs[i:]:
                    receiver = (source + later) % row
                    slots.update(part(receiver, later, direction))
                need[n] = slots
            width = max(max(v) - min(v) + 1 for v in need.values())
            lo = {n: min(min(v), rows_back + 1 - width) for n, v in need.items()}
            send = []
            for z in range(row):
                offset = lo[z] - (0 if held is None else held[(z - direction) % row])
                assert 0 <= offset and offset + width <= (rows_back + 1 if held is None else steps[-1]["width"])
                send.append(offset)
            take, blocks = [], None
            for z in range(row):
                sender = (z - direction) % row
                slots = part(z, b, direction)
                take.append(slots[0] - lo[sender])
                lo_z = 1 if z < b else 0
                mine = [b + row * (m - lo_z) for m in slots]
                assert blocks is None or blocks == mine
                blocks = mine
            steps.append({"dir": direction, "width": width, "send": send, "take": take, "blocks": blocks})
            held = lo
        chains.append(steps)
    return chains, direct


def solution(mesh):
    n_ctx, n_head = mesh.shape["ctx"], mesh.shape["head"]
    row = 8 if n_ctx % 8 == 0 else n_ctx
    placed = (P("ctx", "head"), P("ctx", "head"), P("ctx", "head"), P(), P(None, "head"))
    return jax.shard_map(
        make_body(n_ctx, n_head, row), mesh=mesh, in_specs=placed, out_specs=P("ctx", "head"), check_vma=False
    )
```

```python
import jax
import jax.numpy as jnp
from jax import lax
from jax.sharding import PartitionSpec as P

HD = 128
MOST = 2048


rope_theta = 500000.0


def doc_starts(lengths, positions):
    idx = jnp.arange(lengths.shape[0])
    doc_ends = jnp.sum(jnp.where(idx[None, :] <= idx[:, None], lengths[None, :], 0), axis=1)
    picked = jnp.where(doc_ends[None, :] <= positions[:, None], lengths[None, :], 0)
    return jnp.sum(picked, axis=1)


def rotary(projected, offsets, head_dim):
    token_count = projected.shape[0]
    heads_grid = projected.astype(jnp.float32).reshape(token_count, -1, head_dim)
    half_dim = head_dim // 2
    inverse = rope_theta ** (-2.0 * jnp.arange(half_dim).astype(jnp.float32) / head_dim)
    angles = offsets.astype(jnp.float32)[:, None] * inverse[None, :]
    cosine = jnp.cos(angles)[:, None, :]
    sine_part = jnp.sin(angles)[:, None, :]
    first_half = heads_grid[..., :half_dim]
    second_half = heads_grid[..., half_dim:]
    rotated = jnp.concatenate(
        [
            first_half * cosine - second_half * sine_part,
            second_half * cosine + first_half * sine_part,
        ],
        axis=-1,
    )
    return rotated.reshape(token_count, -1).astype(jnp.bfloat16)


def make_body(n_ctx, n_head, row):
    def on_device(queries, key_proj, value_proj, lengths, out_weight):
        tok_rows = queries.shape[0]
        kv_width = key_proj.shape[1]
        kv_local = kv_width // HD
        query_group = queries.shape[1] // kv_width
        back = -(-(MOST - 1) // tok_rows)
        rows_back = -(-back // row)
        span = rows_back * row
        ctx = lax.axis_index("ctx")
        first_row = ctx * tok_rows
        positions = first_row + jnp.arange(tok_rows, dtype=jnp.int32)
        starts = doc_starts(lengths, positions)
        offsets = positions - starts
        q_rot = rotary(queries, offsets, HD).reshape(tok_rows, kv_local, query_group, HD)
        k_rot = rotary(key_proj, offsets, HD)
        own = jnp.concatenate([k_rot, value_proj], axis=1)

        bundle = [own]
        for m in range(1, rows_back + 1):
            shift = row * m
            bundle.append(lax.ppermute(own, "ctx", [(s, s + shift) for s in range(n_ctx - shift)]))
        blocks = {row * m: bundle[m] for m in range(rows_back + 1)}
        bundle = jnp.stack(bundle)
        z = ctx % row
        n_rows = n_ctx // row
        chains, direct = relay_plan(row, rows_back)
        if direct:
            half = row // 2
            lo = jnp.where((z + half) % row < half, 1, 0)
            got = lax.ppermute(
                lax.dynamic_slice_in_dim(bundle, lo, rows_back, 0),
                "ctx",
                [(r * row + s, r * row + (s + half) % row) for r in range(n_rows) for s in range(row)],
            )
            for m in range(rows_back):
                blocks[half + row * m] = got[m]
        for chain in chains:
            packet = bundle
            for step in chain:
                lo = pick(step["send"], z)
                packet = lax.ppermute(
                    lax.dynamic_slice_in_dim(packet, lo, step["width"], 0),
                    "ctx",
                    [(r * row + s, r * row + (s + step["dir"]) % row) for r in range(n_rows) for s in range(row)],
                )
                at = pick(step["take"], z)
                got = lax.dynamic_slice_in_dim(packet, at, len(step["blocks"]), 0)
                for i, blk in enumerate(step["blocks"]):
                    blocks[blk] = got[i]
        window = jnp.concatenate([blocks[span - k] for k in range(span + 1)], axis=0)
        key_count = window.shape[0]
        key_block = window[:, :kv_width].reshape(key_count, kv_local, HD)
        value_block = window[:, kv_width:].reshape(key_count, kv_local, HD)

        scores = jnp.einsum(
            "tkgd,nkd->kgtn", q_rot, key_block, preferred_element_type=jnp.float32
        ) / jnp.sqrt(jnp.float32(HD))
        key_pos = (ctx - span) * tok_rows + jnp.arange(key_count, dtype=jnp.int32)
        allowed = (key_pos[None, :] <= positions[:, None]) & (key_pos[None, :] >= starts[:, None])
        scores = jnp.where(allowed, scores, -1e30)
        row_max = jnp.max(scores, axis=-1)
        weights = jnp.where(allowed, jnp.exp(scores - row_max[..., None]), 0.0)
        row_sum = jnp.sum(weights, axis=-1)
        weighted = jnp.einsum(
            "kgtn,nkd->kgtd",
            weights.astype(jnp.bfloat16),
            value_block,
            preferred_element_type=jnp.float32,
        )
        normed = (weighted / row_sum[..., None]).astype(jnp.bfloat16)
        attended = jnp.transpose(normed, (2, 0, 1, 3)).reshape(tok_rows, kv_local * query_group * HD)

        feat = attended.shape[1]
        head = lax.axis_index("head")
        core = head % 2

        def project(piece, src):
            rows = lax.dynamic_slice_in_dim(out_weight, src * feat, feat, 0)
            return jnp.dot(piece, rows, preferred_element_type=jnp.float32)

        up = lax.ppermute(attended, "head", [(s, (s + 2) % n_head) for s in range(n_head)])
        down = lax.ppermute(attended, "head", [(s, (s - 2) % n_head) for s in range(n_head)])
        swap = [(s, s ^ 1) for s in range(n_head)]
        partner = lax.ppermute(attended, "head", swap)
        cross = lax.ppermute(attended, "head", [(s, (s + 1) % n_head) if s % 2 else (s, (s - 1) % n_head) for s in range(n_head)])
        same_pairs = [(s, (s + 2) % n_head) if s % 2 == 0 else (s, (s - 2) % n_head) for s in range(n_head)]
        far = lax.ppermute(
            jnp.where(core == 0, jnp.stack([up, cross]), jnp.stack([down, cross])), "head", same_pairs
        )
        other = lax.ppermute(jnp.where(core == 0, up, down), "head", swap)
        total = project(attended, head)
        total = total + project(up, (head - 2) % n_head)
        total = total + project(down, (head + 2) % n_head)
        total = total + project(partner, head ^ 1)
        total = total + project(cross, jnp.where(core == 0, head - 1, head + 1) % n_head)
        total = total + project(far[0], (head + 4) % n_head)
        total = total + project(far[1], jnp.where(core == 0, head + 5, head + 3) % n_head)
        total = total + project(other, jnp.where(core == 0, head + 3, head - 3) % n_head)
        return total.astype(jnp.bfloat16)

    return on_device


def pick(table, z):
    out = jnp.int32(0)
    for i, v in enumerate(table):
        if v:
            out = out + jnp.where(z == i, jnp.int32(v), jnp.int32(0))
    return out


def relay_plan(row, rows_back):
    half = row // 2
    direct = row % 2 == 0 and row > 2
    split = False

    def part(z, b, direction):
        lo = 1 if z < b else 0
        slots = list(range(lo, lo + rows_back))
        if split and b == half:
            cut = (rows_back + 1) // 2
            slots = slots[:cut] if direction == 1 else slots[cut:]
        return slots

    chains = []
    for direction in (1, -1):
        rounds = range(1, (half - 1 if direct else half) + 1) if direction == 1 else range(1, row - 1 - half + 1)
        bs = [r if direction == 1 else row - r for r in rounds]
        steps, held = [], None
        for i, b in enumerate(bs):
            need = {}
            for n in range(row):
                source = (n - direction * i) % row
                slots = set()
                for later in bs[i:]:
                    receiver = (source + later) % row
                    slots.update(part(receiver, later, direction))
                need[n] = slots
            width = max(max(v) - min(v) + 1 for v in need.values())
            lo = {n: min(min(v), rows_back + 1 - width) for n, v in need.items()}
            send = []
            for z in range(row):
                offset = lo[z] - (0 if held is None else held[(z - direction) % row])
                assert 0 <= offset and offset + width <= (rows_back + 1 if held is None else steps[-1]["width"])
                send.append(offset)
            take, blocks = [], None
            for z in range(row):
                sender = (z - direction) % row
                slots = part(z, b, direction)
                take.append(slots[0] - lo[sender])
                lo_z = 1 if z < b else 0
                mine = [b + row * (m - lo_z) for m in slots]
                assert blocks is None or blocks == mine
                blocks = mine
            steps.append({"dir": direction, "width": width, "send": send, "take": take, "blocks": blocks})
            held = lo
        chains.append(steps)
    return chains, direct


def solution(mesh):
    n_ctx, n_head = mesh.shape["ctx"], mesh.shape["head"]
    row = 8 if n_ctx % 8 == 0 else n_ctx
    placed = (P("ctx", "head"), P("ctx", "head"), P("ctx", "head"), P(), P(None, "head"))
    return jax.shard_map(
        make_body(n_ctx, n_head, row), mesh=mesh, in_specs=placed, out_specs=P("ctx", "head"), check_vma=False
    )
```

```python
import jax
import jax.numpy as jnp
from jax import lax
from jax.sharding import PartitionSpec as P

HD = 128
MOST = 2048


rope_theta = 500000.0


def doc_starts(lengths, positions):
    idx = jnp.arange(lengths.shape[0])
    doc_ends = jnp.sum(jnp.where(idx[None, :] <= idx[:, None], lengths[None, :], 0), axis=1)
    picked = jnp.where(doc_ends[None, :] <= positions[:, None], lengths[None, :], 0)
    return jnp.sum(picked, axis=1)


def rotary(projected, offsets, head_dim):
    token_count = projected.shape[0]
    heads_grid = projected.astype(jnp.float32).reshape(token_count, -1, head_dim)
    half_dim = head_dim // 2
    inverse = rope_theta ** (-2.0 * jnp.arange(half_dim).astype(jnp.float32) / head_dim)
    angles = offsets.astype(jnp.float32)[:, None] * inverse[None, :]
    cosine = jnp.cos(angles)[:, None, :]
    sine_part = jnp.sin(angles)[:, None, :]
    first_half = heads_grid[..., :half_dim]
    second_half = heads_grid[..., half_dim:]
    rotated = jnp.concatenate(
        [
            first_half * cosine - second_half * sine_part,
            second_half * cosine + first_half * sine_part,
        ],
        axis=-1,
    )
    return rotated.reshape(token_count, -1).astype(jnp.bfloat16)


def make_body(n_ctx, n_head, row):
    def on_device(queries, key_proj, value_proj, lengths, out_weight):
        tok_rows = queries.shape[0]
        kv_width = key_proj.shape[1]
        kv_local = kv_width // HD
        query_group = queries.shape[1] // kv_width
        back = -(-(MOST - 1) // tok_rows)
        rows_back = -(-back // row)
        span = rows_back * row
        ctx = lax.axis_index("ctx")
        first_row = ctx * tok_rows
        positions = first_row + jnp.arange(tok_rows, dtype=jnp.int32)
        starts = doc_starts(lengths, positions)
        offsets = positions - starts
        q_rot = rotary(queries, offsets, HD).reshape(tok_rows, kv_local, query_group, HD)
        k_rot = rotary(key_proj, offsets, HD)
        own = jnp.concatenate([k_rot, value_proj], axis=1)

        bundle = [own]
        for m in range(1, rows_back + 1):
            shift = row * m
            bundle.append(lax.ppermute(own, "ctx", [(s, s + shift) for s in range(n_ctx - shift)]))
        blocks = {row * m: bundle[m] for m in range(rows_back + 1)}
        bundle = jnp.stack(bundle)
        z = ctx % row
        n_rows = n_ctx // row
        chains, direct = relay_plan(row, rows_back)
        if direct:
            half = row // 2
            lo = jnp.where((z + half) % row < half, 1, 0)
            got = lax.ppermute(
                lax.dynamic_slice_in_dim(bundle, lo, rows_back, 0),
                "ctx",
                [(r * row + s, r * row + (s + half) % row) for r in range(n_rows) for s in range(row)],
            )
            for m in range(rows_back):
                blocks[half + row * m] = got[m]
        for chain in chains:
            packet = bundle
            for step in chain:
                lo = pick(step["send"], z)
                packet = lax.ppermute(
                    lax.dynamic_slice_in_dim(packet, lo, step["width"], 0),
                    "ctx",
                    [(r * row + s, r * row + (s + step["dir"]) % row) for r in range(n_rows) for s in range(row)],
                )
                at = pick(step["take"], z)
                got = lax.dynamic_slice_in_dim(packet, at, len(step["blocks"]), 0)
                for i, blk in enumerate(step["blocks"]):
                    blocks[blk] = got[i]
        window = jnp.concatenate([blocks[span - k] for k in range(span + 1)], axis=0)
        key_count = window.shape[0]
        key_block = window[:, :kv_width].reshape(key_count, kv_local, HD)
        value_block = window[:, kv_width:].reshape(key_count, kv_local, HD)

        scores = jnp.einsum(
            "tkgd,nkd->kgtn", q_rot, key_block, preferred_element_type=jnp.float32
        ) / jnp.sqrt(jnp.float32(HD))
        key_pos = (ctx - span) * tok_rows + jnp.arange(key_count, dtype=jnp.int32)
        allowed = (key_pos[None, :] <= positions[:, None]) & (key_pos[None, :] >= starts[:, None])
        scores = jnp.where(allowed, scores, -1e30)
        row_max = jnp.max(scores, axis=-1)
        weights = jnp.where(allowed, jnp.exp(scores - row_max[..., None]), 0.0)
        row_sum = jnp.sum(weights, axis=-1)
        weighted = jnp.einsum(
            "kgtn,nkd->kgtd",
            weights.astype(jnp.bfloat16),
            value_block,
            preferred_element_type=jnp.float32,
        )
        normed = (weighted / row_sum[..., None]).astype(jnp.bfloat16)
        attended = jnp.transpose(normed, (2, 0, 1, 3)).reshape(tok_rows, kv_local * query_group * HD)

        feat = attended.shape[1]
        head = lax.axis_index("head")
        core = head % 2

        def project(piece, src):
            rows = lax.dynamic_slice_in_dim(out_weight, src * feat, feat, 0)
            return jnp.dot(piece, rows, preferred_element_type=jnp.float32)

        up = lax.ppermute(attended, "head", [(s, (s + 2) % n_head) for s in range(n_head)])
        down = lax.ppermute(attended, "head", [(s, (s - 2) % n_head) for s in range(n_head)])
        swap = [(s, s ^ 1) for s in range(n_head)]
        partner = lax.ppermute(attended, "head", swap)
        same_pairs = [(s, (s + 2) % n_head) if s % 2 == 0 else (s, (s - 2) % n_head) for s in range(n_head)]
        far = lax.ppermute(jnp.where(core == 0, up, down), "head", same_pairs)
        cross_pairs = [(s, (s + 1) % n_head) if s % 2 == 1 else (s, (s - 1) % n_head) for s in range(n_head)]
        far_cross = lax.ppermute(jnp.where(core == 1, up, down), "head", cross_pairs)
        near_other = lax.ppermute(jnp.stack([up, down]), "head", swap)
        other = head ^ 1
        total = project(attended, head)
        total = lax.optimization_barrier(total) + project(up, (head - 2) % n_head)
        total = lax.optimization_barrier(total) + project(down, (head + 2) % n_head)
        total = lax.optimization_barrier(total) + project(partner, other)
        total = lax.optimization_barrier(total) + project(far, (head + 4) % n_head)
        total = lax.optimization_barrier(total) + project(far_cross, jnp.where(core == 0, head - 3, head + 3) % n_head)
        total = lax.optimization_barrier(total) + project(near_other[0], (other - 2) % n_head)
        total = lax.optimization_barrier(total) + project(near_other[1], (other + 2) % n_head)
        return total.astype(jnp.bfloat16)

    return on_device


def pick(table, z):
    out = jnp.int32(0)
    for i, v in enumerate(table):
        if v:
            out = out + jnp.where(z == i, jnp.int32(v), jnp.int32(0))
    return out


def relay_plan(row, rows_back):
    half = row // 2
    direct = row % 2 == 0 and row > 2
    split = False

    def part(z, b, direction):
        lo = 1 if z < b else 0
        slots = list(range(lo, lo + rows_back))
        if split and b == half:
            cut = (rows_back + 1) // 2
            slots = slots[:cut] if direction == 1 else slots[cut:]
        return slots

    chains = []
    for direction in (1, -1):
        rounds = range(1, (half - 1 if direct else half) + 1) if direction == 1 else range(1, row - 1 - half + 1)
        bs = [r if direction == 1 else row - r for r in rounds]
        steps, held = [], None
        for i, b in enumerate(bs):
            need = {}
            for n in range(row):
                source = (n - direction * i) % row
                slots = set()
                for later in bs[i:]:
                    receiver = (source + later) % row
                    slots.update(part(receiver, later, direction))
                need[n] = slots
            width = max(max(v) - min(v) + 1 for v in need.values())
            lo = {n: min(min(v), rows_back + 1 - width) for n, v in need.items()}
            send = []
            for z in range(row):
                offset = lo[z] - (0 if held is None else held[(z - direction) % row])
                assert 0 <= offset and offset + width <= (rows_back + 1 if held is None else steps[-1]["width"])
                send.append(offset)
            take, blocks = [], None
            for z in range(row):
                sender = (z - direction) % row
                slots = part(z, b, direction)
                take.append(slots[0] - lo[sender])
                lo_z = 1 if z < b else 0
                mine = [b + row * (m - lo_z) for m in slots]
                assert blocks is None or blocks == mine
                blocks = mine
            steps.append({"dir": direction, "width": width, "send": send, "take": take, "blocks": blocks})
            held = lo
        chains.append(steps)
    return chains, direct


def solution(mesh):
    n_ctx, n_head = mesh.shape["ctx"], mesh.shape["head"]
    row = 8 if n_ctx % 8 == 0 else n_ctx
    placed = (P("ctx", "head"), P("ctx", "head"), P("ctx", "head"), P(), P(None, "head"))
    return jax.shard_map(
        make_body(n_ctx, n_head, row), mesh=mesh, in_specs=placed, out_specs=P("ctx", "head"), check_vma=False
    )
```

```python
import jax
import jax.numpy as jnp
from jax import lax
from jax.sharding import PartitionSpec as P

HD = 128
MOST = 2048


rope_theta = 500000.0


def doc_starts(lengths, positions):
    idx = jnp.arange(lengths.shape[0])
    doc_ends = jnp.sum(jnp.where(idx[None, :] <= idx[:, None], lengths[None, :], 0), axis=1)
    picked = jnp.where(doc_ends[None, :] <= positions[:, None], lengths[None, :], 0)
    return jnp.sum(picked, axis=1)


def rotary(projected, offsets, head_dim):
    token_count = projected.shape[0]
    heads_grid = projected.astype(jnp.float32).reshape(token_count, -1, head_dim)
    half_dim = head_dim // 2
    inverse = rope_theta ** (-2.0 * jnp.arange(half_dim).astype(jnp.float32) / head_dim)
    angles = offsets.astype(jnp.float32)[:, None] * inverse[None, :]
    cosine = jnp.cos(angles)[:, None, :]
    sine_part = jnp.sin(angles)[:, None, :]
    first_half = heads_grid[..., :half_dim]
    second_half = heads_grid[..., half_dim:]
    rotated = jnp.concatenate(
        [
            first_half * cosine - second_half * sine_part,
            second_half * cosine + first_half * sine_part,
        ],
        axis=-1,
    )
    return rotated.reshape(token_count, -1).astype(jnp.bfloat16)


def make_body(n_ctx, n_head, row):
    def on_device(queries, key_proj, value_proj, lengths, out_weight):
        tok_rows = queries.shape[0]
        kv_width = key_proj.shape[1]
        kv_local = kv_width // HD
        query_group = queries.shape[1] // kv_width
        back = -(-(MOST - 1) // tok_rows)
        rows_back = -(-back // row)
        span = rows_back * row
        ctx = lax.axis_index("ctx")
        first_row = ctx * tok_rows
        positions = first_row + jnp.arange(tok_rows, dtype=jnp.int32)
        starts = doc_starts(lengths, positions)
        offsets = positions - starts
        q_rot = rotary(queries, offsets, HD).reshape(tok_rows, kv_local, query_group, HD)
        k_rot = rotary(key_proj, offsets, HD)
        own = jnp.concatenate([k_rot, value_proj], axis=1)

        bundle = [own]
        for m in range(1, rows_back + 1):
            shift = row * m
            bundle.append(lax.ppermute(own, "ctx", [(s, s + shift) for s in range(n_ctx - shift)]))
        blocks = {row * m: bundle[m] for m in range(rows_back + 1)}
        bundle = jnp.stack(bundle)
        z = ctx % row
        n_rows = n_ctx // row
        chains, direct = relay_plan(row, rows_back)
        if direct:
            half = row // 2
            lo = jnp.where((z + half) % row < half, 1, 0)
            got = lax.ppermute(
                lax.dynamic_slice_in_dim(bundle, lo, rows_back, 0),
                "ctx",
                [(r * row + s, r * row + (s + half) % row) for r in range(n_rows) for s in range(row)],
            )
            for m in range(rows_back):
                blocks[half + row * m] = got[m]
        for chain in chains:
            packet = bundle
            for step in chain:
                lo = pick(step["send"], z)
                packet = lax.ppermute(
                    lax.dynamic_slice_in_dim(packet, lo, step["width"], 0),
                    "ctx",
                    [(r * row + s, r * row + (s + step["dir"]) % row) for r in range(n_rows) for s in range(row)],
                )
                at = pick(step["take"], z)
                got = lax.dynamic_slice_in_dim(packet, at, len(step["blocks"]), 0)
                for i, blk in enumerate(step["blocks"]):
                    blocks[blk] = got[i]
        window = jnp.concatenate([blocks[span - k] for k in range(span + 1)], axis=0)
        key_count = window.shape[0]
        key_block = window[:, :kv_width].reshape(key_count, kv_local, HD)
        value_block = window[:, kv_width:].reshape(key_count, kv_local, HD)

        scores = jnp.einsum(
            "tkgd,nkd->kgtn", q_rot, key_block, preferred_element_type=jnp.float32
        ) / jnp.sqrt(jnp.float32(HD))
        key_pos = (ctx - span) * tok_rows + jnp.arange(key_count, dtype=jnp.int32)
        allowed = (key_pos[None, :] <= positions[:, None]) & (key_pos[None, :] >= starts[:, None])
        scores = jnp.where(allowed, scores, -1e30)
        row_max = jnp.max(scores, axis=-1)
        weights = jnp.exp(scores - row_max[..., None])
        row_sum = jnp.sum(weights, axis=-1)
        weighted = jnp.einsum(
            "kgtn,nkd->kgtd",
            weights.astype(jnp.bfloat16),
            value_block,
            preferred_element_type=jnp.float32,
        )
        normed = (weighted / row_sum[..., None]).astype(jnp.bfloat16)
        attended = jnp.transpose(normed, (2, 0, 1, 3)).reshape(tok_rows, kv_local * query_group * HD)

        feat = attended.shape[1]
        head = lax.axis_index("head")
        core = head % 2

        def project(piece, src):
            rows = lax.dynamic_slice_in_dim(out_weight, src * feat, feat, 0)
            return jnp.dot(piece, rows, preferred_element_type=jnp.float32)

        up = lax.ppermute(attended, "head", [(s, (s + 2) % n_head) for s in range(n_head)])
        down = lax.ppermute(attended, "head", [(s, (s - 2) % n_head) for s in range(n_head)])
        swap = [(s, s ^ 1) for s in range(n_head)]
        partner = lax.ppermute(attended, "head", swap)
        same_pairs = [(s, (s + 2) % n_head) if s % 2 == 0 else (s, (s - 2) % n_head) for s in range(n_head)]
        far = lax.ppermute(jnp.where(core == 0, up, down), "head", same_pairs)
        cross_pairs = [(s, (s + 1) % n_head) if s % 2 == 1 else (s, (s - 1) % n_head) for s in range(n_head)]
        far_cross = lax.ppermute(jnp.where(core == 1, up, down), "head", cross_pairs)
        near_other = lax.ppermute(jnp.stack([up, down]), "head", swap)
        other = head ^ 1
        total = project(attended, head)
        total = total + project(up, (head - 2) % n_head)
        total = total + project(down, (head + 2) % n_head)
        total = total + project(partner, other)
        total = total + project(far, (head + 4) % n_head)
        total = total + project(far_cross, jnp.where(core == 0, head - 3, head + 3) % n_head)
        total = total + project(near_other[0], (other - 2) % n_head)
        total = total + project(near_other[1], (other + 2) % n_head)
        return total.astype(jnp.bfloat16)

    return on_device


def pick(table, z):
    out = jnp.int32(0)
    for i, v in enumerate(table):
        if v:
            out = out + jnp.where(z == i, jnp.int32(v), jnp.int32(0))
    return out


def relay_plan(row, rows_back):
    half = row // 2
    direct = row % 2 == 0 and row > 2
    split = False

    def part(z, b, direction):
        lo = 1 if z < b else 0
        slots = list(range(lo, lo + rows_back))
        if split and b == half:
            cut = (rows_back + 1) // 2
            slots = slots[:cut] if direction == 1 else slots[cut:]
        return slots

    chains = []
    for direction in (1, -1):
        rounds = range(1, (half - 1 if direct else half) + 1) if direction == 1 else range(1, row - 1 - half + 1)
        bs = [r if direction == 1 else row - r for r in rounds]
        steps, held = [], None
        for i, b in enumerate(bs):
            need = {}
            for n in range(row):
                source = (n - direction * i) % row
                slots = set()
                for later in bs[i:]:
                    receiver = (source + later) % row
                    slots.update(part(receiver, later, direction))
                need[n] = slots
            width = max(max(v) - min(v) + 1 for v in need.values())
            lo = {n: min(min(v), rows_back + 1 - width) for n, v in need.items()}
            send = []
            for z in range(row):
                offset = lo[z] - (0 if held is None else held[(z - direction) % row])
                assert 0 <= offset and offset + width <= (rows_back + 1 if held is None else steps[-1]["width"])
                send.append(offset)
            take, blocks = [], None
            for z in range(row):
                sender = (z - direction) % row
                slots = part(z, b, direction)
                take.append(slots[0] - lo[sender])
                lo_z = 1 if z < b else 0
                mine = [b + row * (m - lo_z) for m in slots]
                assert blocks is None or blocks == mine
                blocks = mine
            steps.append({"dir": direction, "width": width, "send": send, "take": take, "blocks": blocks})
            held = lo
        chains.append(steps)
    return chains, direct


def solution(mesh):
    n_ctx, n_head = mesh.shape["ctx"], mesh.shape["head"]
    row = 8 if n_ctx % 8 == 0 else n_ctx
    placed = (P("ctx", "head"), P("ctx", "head"), P("ctx", "head"), P(), P(None, "head"))
    return jax.shard_map(
        make_body(n_ctx, n_head, row), mesh=mesh, in_specs=placed, out_specs=P("ctx", "head"), check_vma=False
    )
```

```python
import jax
import jax.numpy as jnp
from jax import lax
from jax.sharding import PartitionSpec as P

HD = 128
MOST = 2048


rope_theta = 500000.0


def doc_starts(lengths, positions):
    idx = jnp.arange(lengths.shape[0])
    doc_ends = jnp.sum(jnp.where(idx[None, :] <= idx[:, None], lengths[None, :], 0), axis=1)
    picked = jnp.where(doc_ends[None, :] <= positions[:, None], lengths[None, :], 0)
    return jnp.sum(picked, axis=1)


def rotary(projected, offsets, head_dim):
    token_count = projected.shape[0]
    heads_grid = projected.astype(jnp.float32).reshape(token_count, -1, head_dim)
    half_dim = head_dim // 2
    inverse = rope_theta ** (-2.0 * jnp.arange(half_dim).astype(jnp.float32) / head_dim)
    angles = offsets.astype(jnp.float32)[:, None] * inverse[None, :]
    cosine = jnp.cos(angles)[:, None, :]
    sine_part = jnp.sin(angles)[:, None, :]
    first_half = heads_grid[..., :half_dim]
    second_half = heads_grid[..., half_dim:]
    rotated = jnp.concatenate(
        [
            first_half * cosine - second_half * sine_part,
            second_half * cosine + first_half * sine_part,
        ],
        axis=-1,
    )
    return rotated.reshape(token_count, -1).astype(jnp.bfloat16)


def make_body(n_ctx, n_head, row):
    def on_device(queries, key_proj, value_proj, lengths, out_weight):
        tok_rows = queries.shape[0]
        kv_width = key_proj.shape[1]
        kv_local = kv_width // HD
        query_group = queries.shape[1] // kv_width
        back = -(-(MOST - 1) // tok_rows)
        rows_back = -(-back // row)
        span = rows_back * row
        ctx = lax.axis_index("ctx")
        first_row = ctx * tok_rows
        positions = first_row + jnp.arange(tok_rows, dtype=jnp.int32)
        starts = doc_starts(lengths, positions)
        offsets = positions - starts
        q_rot = rotary(queries, offsets, HD).reshape(tok_rows, kv_local, query_group, HD)
        k_rot = rotary(key_proj, offsets, HD)
        own = jnp.concatenate([k_rot, value_proj], axis=1)

        bundle = [own]
        for m in range(1, rows_back + 1):
            shift = row * m
            bundle.append(lax.ppermute(own, "ctx", [(s, s + shift) for s in range(n_ctx - shift)]))
        blocks = {row * m: bundle[m] for m in range(rows_back + 1)}
        bundle = jnp.stack(bundle)
        z = ctx % row
        n_rows = n_ctx // row
        chains, direct = relay_plan(row, rows_back)
        late = []
        if direct:
            half = row // 2
            lo = jnp.where((z + half) % row < half, 1, 0)
            got = lax.ppermute(
                lax.dynamic_slice_in_dim(bundle, lo, rows_back, 0),
                "ctx",
                [(r * row + s, r * row + (s + half) % row) for r in range(n_rows) for s in range(row)],
            )
            for m in range(rows_back):
                blocks[half + row * m] = got[m]
                late.append(half + row * m)
        for chain in chains:
            packet = bundle
            for step in chain:
                lo = pick(step["send"], z)
                packet = lax.ppermute(
                    lax.dynamic_slice_in_dim(packet, lo, step["width"], 0),
                    "ctx",
                    [(r * row + s, r * row + (s + step["dir"]) % row) for r in range(n_rows) for s in range(row)],
                )
                at = pick(step["take"], z)
                got = lax.dynamic_slice_in_dim(packet, at, len(step["blocks"]), 0)
                for i, blk in enumerate(step["blocks"]):
                    blocks[blk] = got[i]
                    if step is chain[-1]:
                        late.append(blk)
        def scored(backs):
            window = jnp.concatenate([blocks[b] for b in backs], axis=0)
            key_count = window.shape[0]
            key_block = window[:, :kv_width].reshape(key_count, kv_local, HD)
            value_block = window[:, kv_width:].reshape(key_count, kv_local, HD)
            scores = jnp.einsum(
                "tkgd,nkd->kgtn", q_rot, key_block, preferred_element_type=jnp.float32
            ) / jnp.sqrt(jnp.float32(HD))
            key_pos = jnp.concatenate(
                [(ctx - b) * tok_rows + jnp.arange(tok_rows, dtype=jnp.int32) for b in backs]
            )
            allowed = (key_pos[None, :] <= positions[:, None]) & (key_pos[None, :] >= starts[:, None])
            return jnp.where(allowed, scores, -1e30), value_block

        early = [b for b in range(span + 1) if b not in late]
        parts = [scored(early), scored(sorted(late))]
        row_max = jnp.maximum(jnp.max(parts[0][0], axis=-1), jnp.max(parts[1][0], axis=-1))
        row_sum = 0.0
        weighted = 0.0
        for scores, value_block in parts:
            weights = jnp.exp(scores - row_max[..., None])
            row_sum = row_sum + jnp.sum(weights, axis=-1)
            weighted = weighted + jnp.einsum(
                "kgtn,nkd->kgtd",
                weights.astype(jnp.bfloat16),
                value_block,
                preferred_element_type=jnp.float32,
            )
        normed = (weighted / row_sum[..., None]).astype(jnp.bfloat16)
        attended = jnp.transpose(normed, (2, 0, 1, 3)).reshape(tok_rows, kv_local * query_group * HD)

        feat = attended.shape[1]
        head = lax.axis_index("head")
        core = head % 2

        def project(piece, src):
            rows = lax.dynamic_slice_in_dim(out_weight, src * feat, feat, 0)
            return jnp.dot(piece, rows, preferred_element_type=jnp.float32)

        up = lax.ppermute(attended, "head", [(s, (s + 2) % n_head) for s in range(n_head)])
        down = lax.ppermute(attended, "head", [(s, (s - 2) % n_head) for s in range(n_head)])
        swap = [(s, s ^ 1) for s in range(n_head)]
        partner = lax.ppermute(attended, "head", swap)
        same_pairs = [(s, (s + 2) % n_head) if s % 2 == 0 else (s, (s - 2) % n_head) for s in range(n_head)]
        far = lax.ppermute(jnp.where(core == 0, up, down), "head", same_pairs)
        cross_pairs = [(s, (s + 1) % n_head) if s % 2 == 1 else (s, (s - 1) % n_head) for s in range(n_head)]
        far_cross = lax.ppermute(jnp.where(core == 1, up, down), "head", cross_pairs)
        near_other = lax.ppermute(jnp.stack([up, down]), "head", swap)
        other = head ^ 1
        total = project(attended, head)
        total = total + project(up, (head - 2) % n_head)
        total = total + project(down, (head + 2) % n_head)
        total = total + project(partner, other)
        total = total + project(far, (head + 4) % n_head)
        total = total + project(far_cross, jnp.where(core == 0, head - 3, head + 3) % n_head)
        total = total + project(near_other[0], (other - 2) % n_head)
        total = total + project(near_other[1], (other + 2) % n_head)
        return total.astype(jnp.bfloat16)

    return on_device


def pick(table, z):
    out = jnp.int32(0)
    for i, v in enumerate(table):
        if v:
            out = out + jnp.where(z == i, jnp.int32(v), jnp.int32(0))
    return out


def relay_plan(row, rows_back):
    half = row // 2
    direct = row % 2 == 0 and row > 2
    split = False

    def part(z, b, direction):
        lo = 1 if z < b else 0
        slots = list(range(lo, lo + rows_back))
        if split and b == half:
            cut = (rows_back + 1) // 2
            slots = slots[:cut] if direction == 1 else slots[cut:]
        return slots

    chains = []
    for direction in (1, -1):
        rounds = range(1, (half - 1 if direct else half) + 1) if direction == 1 else range(1, row - 1 - half + 1)
        bs = [r if direction == 1 else row - r for r in rounds]
        steps, held = [], None
        for i, b in enumerate(bs):
            need = {}
            for n in range(row):
                source = (n - direction * i) % row
                slots = set()
                for later in bs[i:]:
                    receiver = (source + later) % row
                    slots.update(part(receiver, later, direction))
                need[n] = slots
            width = max(max(v) - min(v) + 1 for v in need.values())
            lo = {n: min(min(v), rows_back + 1 - width) for n, v in need.items()}
            send = []
            for z in range(row):
                offset = lo[z] - (0 if held is None else held[(z - direction) % row])
                assert 0 <= offset and offset + width <= (rows_back + 1 if held is None else steps[-1]["width"])
                send.append(offset)
            take, blocks = [], None
            for z in range(row):
                sender = (z - direction) % row
                slots = part(z, b, direction)
                take.append(slots[0] - lo[sender])
                lo_z = 1 if z < b else 0
                mine = [b + row * (m - lo_z) for m in slots]
                assert blocks is None or blocks == mine
                blocks = mine
            steps.append({"dir": direction, "width": width, "send": send, "take": take, "blocks": blocks})
            held = lo
        chains.append(steps)
    return chains, direct


def solution(mesh):
    n_ctx, n_head = mesh.shape["ctx"], mesh.shape["head"]
    row = 8 if n_ctx % 8 == 0 else n_ctx
    placed = (P("ctx", "head"), P("ctx", "head"), P("ctx", "head"), P(), P(None, "head"))
    return jax.shard_map(
        make_body(n_ctx, n_head, row), mesh=mesh, in_specs=placed, out_specs=P("ctx", "head"), check_vma=False
    )
```
